512 devices in a mesh: bits: 32 (over y_hi, z, core), cuts: 16 (over x, y_lo).
Axes of the slice: x: 4, y: 8 (y_hi: 2, y_lo: 4; y = y_hi * 4 + y_lo), z: 8, core: 2. Of those that a mesh axis runs over, the one named last changes fastest.
Arguments:
- boundary: float32 [16, 65536, 128], P('cuts', 'bits'), may hold values from -6 to 6
- gate_stack: float32 [34, 128, 128], replicated, may hold values from -0.5 to 0.5
- coupling: float32 [13, 128, 128], replicated, may hold values from 0.4 to 1.6
Outputs:
- probs: float32 [65536, 128], P('bits', 'cuts')
The draws below stay inside these ranges and needn't reach their ends.
All inputs are finite; a program needn't handle non-finite values.
Results may differ from the reference program's by a relative error of at most 0.00018.
Values sent between devices are 32-bit elements; how exact they have to be, the bound alone decides.
No kernel may reach another device: no remote copies, remote signals or barrier semaphores. Data moves between devices by JAX's collectives and lax.ppermute only.
A program may use at most 64 MiB of HBM per device.

```python
import jax
import jax.numpy as jnp
from jax import lax

GATE = 128
ROWS = 2048
CYC_A = 4
CYC_B = 4
CYC_C = 5
GATES_ALL = 34
CPL_ALL = 13
ROWS_ALL = 65536
SLICES = 16
N_BITS = 32


def block_levels(own_key, dims, split, least, top_value):
    def one(position, blocks):
        steps = jax.random.uniform(jax.random.fold_in(jax.random.fold_in(own_key, 6), position), (blocks,), jnp.float32, least / len(split), top_value / len(split))
        return jnp.repeat(jnp.exp(steps), dims[position] // blocks).reshape((-1,) + (1,) * (len(dims) - position - 1))

    loudness = one(*split[0])
    for cut in split[1:]:
        loudness = loudness * one(*cut)
    return loudness


def normal_values(rng, shape, deviation, reach, cuts=(), kind=jnp.bfloat16):
    drawn = jax.random.normal(rng, shape, jnp.float32) * deviation
    if len(cuts) > 0:
        drawn = block_levels(rng, shape, cuts, -0.22, 0.18) * drawn
    return jnp.clip(drawn, min=-reach, max=reach).astype(kind)


def setup_inputs(seed: int = 0) -> dict:
    splits = jax.random.split(jax.random.key(seed), 4)
    return {
        "boundary": normal_values(splits[0], (SLICES, ROWS_ALL, GATE), 1.0, 6.0, ((0, 16), (1, 32)), jnp.float32),
        "gate_stack": normal_values(splits[1], (GATES_ALL, GATE, GATE), GATE ** -0.5, 0.5, (), jnp.float32),
        "coupling": jnp.clip(jax.random.uniform(splits[2], (CPL_ALL, GATE, GATE), jnp.float32, 0.4, 1.6), 0.4, 1.6),
    }


HIGHEST_PREC = lax.Precision.HIGHEST


def effective(weight_mat):
    order_size = weight_mat.shape[0]
    return 0.9 * jnp.eye(order_size, dtype=weight_mat.dtype) + 0.45 * weight_mat


def apply_lane(tensor, weight_mat):
    return jnp.dot(tensor, effective(weight_mat), precision=HIGHEST_PREC)


def apply_mid(tensor, weight_mat):
    order_size = weight_mat.shape[0]
    shaped = tensor.reshape(-1, order_size, tensor.shape[1])
    mixed = jnp.einsum("aic,ij->ajc", shaped, effective(weight_mat), precision=HIGHEST_PREC)
    return mixed.reshape(tensor.shape)


def apply_top(tensor, weight_mat, blocks):
    order_size = weight_mat.shape[0]
    shaped = tensor.reshape(blocks, order_size, -1)
    mixed = jnp.einsum("bir,ij->bjr", shaped, effective(weight_mat), precision=HIGHEST_PREC)
    return mixed.reshape(tensor.shape)


def apply_couple(tensor, table):
    shaped = tensor.reshape(-1, table.shape[0], tensor.shape[1])
    return (shaped * table[None]).reshape(tensor.shape)


def layer_group(tensor, gate_stack, coupling, gate_base, cpl_base, cycles, blocks):
    for turn_index in range(cycles):
        first = gate_base + 3 * turn_index
        tensor = apply_top(tensor, gate_stack[first], blocks)
        tensor = apply_lane(tensor, gate_stack[first + 1])
        tensor = apply_couple(tensor, coupling[cpl_base + turn_index])
        tensor = apply_mid(tensor, gate_stack[first + 2])
    return tensor


def final_group(tensor, gate_stack, coupling, blocks):
    gate_base = 3 * CYC_A + 3 * CYC_B
    cpl_base = CYC_A + CYC_B
    for turn_index in range(CYC_C):
        tensor = apply_top(tensor, gate_stack[gate_base + 2 * turn_index], blocks)
        tensor = apply_couple(tensor, coupling[cpl_base + turn_index])
        tensor = apply_mid(tensor, gate_stack[gate_base + 2 * turn_index + 1])
    return tensor


def swap_whole(tensor, bit_pos):
    cols = tensor.shape[1]
    shaped = tensor.reshape(N_BITS // (2 * 2 ** bit_pos), 2, 2 ** bit_pos, 2, ROWS // 2, cols)
    return jnp.swapaxes(shaped, 1, 3).reshape(tensor.shape)


def reference(boundary, gate_stack, coupling):
    top_bit = N_BITS.bit_length() - 2

    def one_slice(slice_idx, total):
        tensor = boundary[slice_idx]
        tensor = layer_group(tensor, gate_stack, coupling, 0, 0, CYC_A, N_BITS)
        tensor = swap_whole(tensor, top_bit)
        tensor = layer_group(tensor, gate_stack, coupling, 3 * CYC_A, CYC_A, CYC_B, N_BITS)
        tensor = swap_whole(tensor, 0)
        return total + tensor

    summed = lax.fori_loop(0, SLICES, one_slice, jnp.zeros(boundary.shape[1:], boundary.dtype))
    return final_group(summed, gate_stack, coupling, N_BITS)
```

```python
import jax
import jax.numpy as jnp
from jax import lax
from jax.sharding import PartitionSpec as P

CYC_A = 4
CYC_B = 4
CYC_C = 5


HIGHEST_PREC = lax.Precision.HIGHEST


def partner(value, axis, distance):
    mask = 2**distance
    pairs = [(source, source ^ mask) for source in range(lax.axis_size(axis))]
    return lax.ppermute(value, axis, pairs)


def effective(weight_mat):
    order_size = weight_mat.shape[0]
    return 0.9 * jnp.eye(order_size, dtype=weight_mat.dtype) + 0.45 * weight_mat


def apply_lane(tensor, weight_mat):
    return jnp.dot(tensor, effective(weight_mat), precision=HIGHEST_PREC)


def apply_mid(tensor, weight_mat):
    order_size = weight_mat.shape[0]
    shaped = tensor.reshape(-1, order_size, tensor.shape[1])
    mixed = jnp.einsum("aic,ij->ajc", shaped, effective(weight_mat), precision=HIGHEST_PREC)
    return mixed.reshape(tensor.shape)


def apply_top(tensor, weight_mat):
    order_size = weight_mat.shape[0]
    shaped = tensor.reshape(order_size, -1)
    mixed = jnp.dot(effective(weight_mat).T, shaped, precision=HIGHEST_PREC)
    return mixed.reshape(tensor.shape)


def apply_couple(tensor, table):
    shaped = tensor.reshape(-1, table.shape[0], tensor.shape[1])
    return (shaped * table[None]).reshape(tensor.shape)


def layer_group(tensor, gate_stack, coupling, gate_base, cpl_base, cycles):
    for turn_index in range(cycles):
        first = gate_base + 3 * turn_index
        tensor = apply_top(tensor, gate_stack[first])
        tensor = apply_lane(tensor, gate_stack[first + 1])
        tensor = apply_couple(tensor, coupling[cpl_base + turn_index])
        tensor = apply_mid(tensor, gate_stack[first + 2])
    return tensor


def final_group_cols(cols, gate_stack, coupling, col_start):
    order_size = gate_stack.shape[1]
    width = cols.shape[0]
    gate_base = 3 * CYC_A + 3 * CYC_B
    cpl_base = CYC_A + CYC_B
    for turn_index in range(CYC_C):
        top_mat = effective(gate_stack[gate_base + 2 * turn_index])
        shaped = cols.reshape(width, order_size, -1)
        cols = jnp.einsum("cit,ij->cjt", shaped, top_mat, precision=HIGHEST_PREC).reshape(cols.shape)
        table = lax.dynamic_slice_in_dim(coupling[cpl_base + turn_index], col_start, width, axis=1)
        shaped = cols.reshape(width, -1, order_size)
        cols = (shaped * table.T[:, None, :]).reshape(cols.shape)
        mid_mat = effective(gate_stack[gate_base + 2 * turn_index + 1])
        cols = jnp.dot(cols.reshape(-1, order_size), mid_mat, precision=HIGHEST_PREC).reshape(cols.shape)
    return cols


def swap_bit(tensor, bit_pos):
    half_rows = tensor.shape[0] // 2
    lower = tensor[:half_rows]
    upper = tensor[half_rows:]
    parity = lax.axis_index("bits") >> bit_pos & 1
    outgoing = jnp.where(parity == 0, upper, lower)
    incoming = partner(outgoing, "bits", bit_pos)
    return jnp.where(
        parity == 0, jnp.concatenate([lower, incoming], 0), jnp.concatenate([incoming, upper], 0)
    )


def reduce_columns(tensor):
    n_cuts = lax.axis_size("cuts")
    blocks = tensor.T.reshape(n_cuts, tensor.shape[1] // n_cuts, tensor.shape[0])
    gathered = lax.all_to_all(blocks, "cuts", 0, 0, tiled=False)
    return gathered.sum(0)


def on_device(boundary, gate_stack, coupling):
    tensor = boundary[0]
    top_bit = lax.axis_size("bits").bit_length() - 2
    tensor = layer_group(tensor, gate_stack, coupling, 0, 0, CYC_A)
    tensor = swap_bit(tensor, top_bit)
    tensor = layer_group(tensor, gate_stack, coupling, 3 * CYC_A, CYC_A, CYC_B)
    cols = reduce_columns(tensor)
    cols = swap_bit(cols.T, 0).T
    col_start = lax.axis_index("cuts") * cols.shape[0]
    cols = final_group_cols(cols, gate_stack, coupling, col_start)
    return cols.T


def solution(mesh):
    in_specs = (P("cuts", "bits", None), P(), P())
    out_specs = P("bits", "cuts")
    return jax.shard_map(
        on_device, mesh=mesh, in_specs=in_specs, out_specs=out_specs, check_vma=False
    )
```

```python
import jax
import jax.numpy as jnp
from jax import lax
from jax.sharding import Mesh, PartitionSpec as P

CYC_A = 4
CYC_B = 4
CYC_C = 5
BITS = ("yh", "z", "core")
CUTS = ("x", "yl")


HIGHEST_PREC = lax.Precision.HIGHEST


def partner(value, axis, distance):
    mask = 2**distance
    pairs = [(source, source ^ mask) for source in range(lax.axis_size(axis))]
    return lax.ppermute(value, axis, pairs)


def effective(weight_mat):
    order_size = weight_mat.shape[0]
    return 0.9 * jnp.eye(order_size, dtype=weight_mat.dtype) + 0.45 * weight_mat


def apply_lane(tensor, weight_mat):
    return jnp.dot(tensor, effective(weight_mat), precision=HIGHEST_PREC)


def apply_mid(tensor, weight_mat):
    order_size = weight_mat.shape[0]
    shaped = tensor.reshape(-1, order_size, tensor.shape[1])
    mixed = jnp.einsum("aic,ij->ajc", shaped, effective(weight_mat), precision=HIGHEST_PREC)
    return mixed.reshape(tensor.shape)


def apply_top(tensor, weight_mat):
    order_size = weight_mat.shape[0]
    shaped = tensor.reshape(order_size, -1)
    mixed = jnp.dot(effective(weight_mat).T, shaped, precision=HIGHEST_PREC)
    return mixed.reshape(tensor.shape)


def apply_couple(tensor, table):
    shaped = tensor.reshape(-1, table.shape[0], tensor.shape[1])
    return (shaped * table[None]).reshape(tensor.shape)


def layer_group(tensor, gate_stack, coupling, gate_base, cpl_base, cycles):
    for turn_index in range(cycles):
        first = gate_base + 3 * turn_index
        tensor = apply_top(tensor, gate_stack[first])
        tensor = apply_lane(tensor, gate_stack[first + 1])
        tensor = apply_couple(tensor, coupling[cpl_base + turn_index])
        tensor = apply_mid(tensor, gate_stack[first + 2])
    return tensor


def final_group_cols(cols, gate_stack, coupling, col_start):
    order_size = gate_stack.shape[1]
    width = cols.shape[0]
    gate_base = 3 * CYC_A + 3 * CYC_B
    cpl_base = CYC_A + CYC_B
    for turn_index in range(CYC_C):
        top_mat = effective(gate_stack[gate_base + 2 * turn_index])
        shaped = cols.reshape(width, order_size, -1)
        cols = jnp.einsum("cit,ij->cjt", shaped, top_mat, precision=HIGHEST_PREC).reshape(cols.shape)
        table = lax.dynamic_slice_in_dim(coupling[cpl_base + turn_index], col_start, width, axis=1)
        shaped = cols.reshape(width, -1, order_size)
        cols = (shaped * table.T[:, None, :]).reshape(cols.shape)
        mid_mat = effective(gate_stack[gate_base + 2 * turn_index + 1])
        cols = jnp.dot(cols.reshape(-1, order_size), mid_mat, precision=HIGHEST_PREC).reshape(cols.shape)
    return cols


def swap_bit(tensor, bit_pos):
    half_rows = tensor.shape[0] // 2
    lower = tensor[:half_rows]
    upper = tensor[half_rows:]
    parity = lax.axis_index(BITS) >> bit_pos & 1
    outgoing = jnp.where(parity == 0, upper, lower)
    incoming = partner(outgoing, BITS, bit_pos)
    return jnp.where(
        parity == 0, jnp.concatenate([lower, incoming], 0), jnp.concatenate([incoming, upper], 0)
    )


def reduce_columns(tensor):
    cols = tensor.T
    for axis in ("x", "yl"):
        n = lax.axis_size(axis)
        blocks = cols.reshape(n, cols.shape[0] // n, cols.shape[1])
        cols = lax.all_to_all(blocks, axis, 0, 0, tiled=False).sum(0)
    return cols


def on_device(boundary, gate_stack, coupling):
    tensor = boundary[0]
    top_bit = lax.axis_size(BITS).bit_length() - 2
    tensor = layer_group(tensor, gate_stack, coupling, 0, 0, CYC_A)
    tensor = swap_bit(tensor, top_bit)
    tensor = layer_group(tensor, gate_stack, coupling, 3 * CYC_A, CYC_A, CYC_B)
    cols = reduce_columns(tensor)
    cols = swap_bit(cols.T, 0).T
    col_start = lax.axis_index(CUTS) * cols.shape[0]
    cols = final_group_cols(cols, gate_stack, coupling, col_start)
    return cols.T


def solution(mesh):
    n_bits, n_cuts = mesh.shape["bits"], mesh.shape["cuts"]
    fine = Mesh(mesh.devices.reshape(2, n_bits // 4, 2, n_cuts // 4, 4), BITS + CUTS)
    in_specs = (P(CUTS, BITS, None), P(), P())
    out_specs = P(BITS, CUTS)
    return jax.shard_map(
        on_device, mesh=fine, in_specs=in_specs, out_specs=out_specs, check_vma=False
    )
```

```python
import functools

import jax
import jax.numpy as jnp
from jax import lax
from jax.experimental import pallas as pl
from jax.sharding import Mesh, PartitionSpec as P

CYC_A = 4
CYC_B = 4
CYC_C = 5
BITS = ("yh", "z", "core")
CUTS = ("x", "yl")

BLOCK = 128


def _split(a):
    hi = a.astype(jnp.bfloat16)
    lo = (a - hi.astype(jnp.float32)).astype(jnp.bfloat16)
    return hi, lo


def _mm3(a, b):
    dot = functools.partial(jnp.dot, preferred_element_type=jnp.float32)
    return dot(a[0], b[0]) + (dot(a[1], b[0]) + dot(a[0], b[1]))


def _layers_kernel(x_ref, g_ref, c_ref, o_ref, *, gate_base, cpl_base, cycles):
    rows = x_ref.shape[0]
    n_blocks = rows // BLOCK
    stride = rows // BLOCK
    o_ref[...] = x_ref[...]
    for turn in range(cycles):
        first = gate_base + 3 * turn
        top_t = _split((0.45 * g_ref[first]).T)
        lane_g = _split(0.45 * g_ref[first + 1])
        mid_t = _split((0.45 * g_ref[first + 2]).T)
        table = c_ref[cpl_base + turn]

        def top(t, carry):
            rows_t = pl.ds(t, BLOCK, stride=stride)
            xt = o_ref[rows_t, :]
            o_ref[rows_t, :] = 0.9 * xt + _mm3(top_t, _split(xt))
            return carry

        lax.fori_loop(0, stride, top, 0)

        def lane_mid(a, carry):
            rows_a = pl.ds(pl.multiple_of(a * BLOCK, BLOCK), BLOCK)
            xa = o_ref[rows_a, :]
            xa = (0.9 * xa + _mm3(_split(xa), lane_g)) * table
            o_ref[rows_a, :] = 0.9 * xa + _mm3(mid_t, _split(xa))
            return carry

        lax.fori_loop(0, n_blocks, lane_mid, 0)


def layers(x, gate_stack, coupling, gate_base, cpl_base, cycles):
    kernel = functools.partial(_layers_kernel, gate_base=gate_base, cpl_base=cpl_base, cycles=cycles)
    return pl.pallas_call(
        kernel,
        out_shape=jax.ShapeDtypeStruct(x.shape, x.dtype),
    )(x, gate_stack, coupling)


HIGHEST_PREC = lax.Precision.HIGHEST


def partner(value, axis, distance):
    mask = 2**distance
    pairs = [(source, source ^ mask) for source in range(lax.axis_size(axis))]
    return lax.ppermute(value, axis, pairs)


def effective(weight_mat):
    order_size = weight_mat.shape[0]
    return 0.9 * jnp.eye(order_size, dtype=weight_mat.dtype) + 0.45 * weight_mat


def apply_lane(tensor, weight_mat):
    return jnp.dot(tensor, effective(weight_mat), precision=HIGHEST_PREC)


def apply_mid(tensor, weight_mat):
    order_size = weight_mat.shape[0]
    shaped = tensor.reshape(-1, order_size, tensor.shape[1])
    mixed = jnp.einsum("aic,ij->ajc", shaped, effective(weight_mat), precision=HIGHEST_PREC)
    return mixed.reshape(tensor.shape)


def apply_top(tensor, weight_mat):
    order_size = weight_mat.shape[0]
    shaped = tensor.reshape(order_size, -1)
    mixed = jnp.dot(effective(weight_mat).T, shaped, precision=HIGHEST_PREC)
    return mixed.reshape(tensor.shape)


def apply_couple(tensor, table):
    shaped = tensor.reshape(-1, table.shape[0], tensor.shape[1])
    return (shaped * table[None]).reshape(tensor.shape)


def layer_group(tensor, gate_stack, coupling, gate_base, cpl_base, cycles):
    for turn_index in range(cycles):
        first = gate_base + 3 * turn_index
        tensor = apply_top(tensor, gate_stack[first])
        tensor = apply_lane(tensor, gate_stack[first + 1])
        tensor = apply_couple(tensor, coupling[cpl_base + turn_index])
        tensor = apply_mid(tensor, gate_stack[first + 2])
    return tensor


def final_group_cols(cols, gate_stack, coupling, col_start):
    order_size = gate_stack.shape[1]
    width = cols.shape[0]
    gate_base = 3 * CYC_A + 3 * CYC_B
    cpl_base = CYC_A + CYC_B
    for turn_index in range(CYC_C):
        top_mat = effective(gate_stack[gate_base + 2 * turn_index])
        shaped = cols.reshape(width, order_size, -1)
        cols = jnp.einsum("cit,ij->cjt", shaped, top_mat, precision=HIGHEST_PREC).reshape(cols.shape)
        table = lax.dynamic_slice_in_dim(coupling[cpl_base + turn_index], col_start, width, axis=1)
        shaped = cols.reshape(width, -1, order_size)
        cols = (shaped * table.T[:, None, :]).reshape(cols.shape)
        mid_mat = effective(gate_stack[gate_base + 2 * turn_index + 1])
        cols = jnp.dot(cols.reshape(-1, order_size), mid_mat, precision=HIGHEST_PREC).reshape(cols.shape)
    return cols


def swap_bit(tensor, bit_pos):
    half_rows = tensor.shape[0] // 2
    lower = tensor[:half_rows]
    upper = tensor[half_rows:]
    parity = lax.axis_index(BITS) >> bit_pos & 1
    outgoing = jnp.where(parity == 0, upper, lower)
    incoming = partner(outgoing, BITS, bit_pos)
    return jnp.where(
        parity == 0, jnp.concatenate([lower, incoming], 0), jnp.concatenate([incoming, upper], 0)
    )


def reduce_columns(tensor):
    cols = tensor.T
    for axis in ("x", "yl"):
        n = lax.axis_size(axis)
        blocks = cols.reshape(n, cols.shape[0] // n, cols.shape[1])
        cols = lax.all_to_all(blocks, axis, 0, 0, tiled=False).sum(0)
    return cols


def on_device(boundary, gate_stack, coupling):
    tensor = boundary[0]
    top_bit = lax.axis_size(BITS).bit_length() - 2
    tensor = layers(tensor, gate_stack, coupling, 0, 0, CYC_A)
    tensor = swap_bit(tensor, top_bit)
    tensor = layers(tensor, gate_stack, coupling, 3 * CYC_A, CYC_A, CYC_B)
    cols = reduce_columns(tensor)
    cols = swap_bit(cols.T, 0).T
    col_start = lax.axis_index(CUTS) * cols.shape[0]
    cols = final_group_cols(cols, gate_stack, coupling, col_start)
    return cols.T


def solution(mesh):
    n_bits, n_cuts = mesh.shape["bits"], mesh.shape["cuts"]
    fine = Mesh(mesh.devices.reshape(2, n_bits // 4, 2, n_cuts // 4, 4), BITS + CUTS)
    in_specs = (P(CUTS, BITS, None), P(), P())
    out_specs = P(BITS, CUTS)
    return jax.shard_map(
        on_device, mesh=fine, in_specs=in_specs, out_specs=out_specs, check_vma=False
    )
```

```python
import functools

import jax
import jax.numpy as jnp
from jax import lax
from jax.experimental import pallas as pl
from jax.experimental.pallas import tpu as pltpu
from jax.sharding import Mesh, PartitionSpec as P

CYC_A = 4
CYC_B = 4
CYC_C = 5
BITS = ("yh", "z", "core")
CUTS = ("x", "yl")

BLOCK = 128


def _split(a):
    hi = a.astype(jnp.bfloat16)
    lo = (a - hi.astype(jnp.float32)).astype(jnp.bfloat16)
    return hi, lo


def _weights(g):
    hi, lo = _split(0.45 * g)
    return jnp.concatenate([hi, hi, lo], axis=0)


def _apply(x, w):
    hi, lo = _split(x)
    lhs = jnp.concatenate([hi, lo, hi], axis=1)
    return 0.9 * x + jnp.dot(lhs, w, preferred_element_type=jnp.float32)


def _layers_kernel(x_ref, g_ref, c_ref, o_ref, t_ref, *, gate_base, cpl_base, cycles):
    rows = x_ref.shape[0]
    n_blocks = rows // BLOCK
    o_ref[...] = x_ref[...]
    for turn in range(cycles):
        first = gate_base + 3 * turn
        table = c_ref[cpl_base + turn]
        for t in range(n_blocks):
            t_ref[pl.ds(t * BLOCK, BLOCK), :] = o_ref[pl.ds(t, BLOCK, stride=n_blocks), :].T
        t_ref[...] = _apply(t_ref[...], _weights(g_ref[first]))
        for t in range(n_blocks):
            o_ref[pl.ds(t, BLOCK, stride=n_blocks), :] = t_ref[pl.ds(t * BLOCK, BLOCK), :].T
        y = _apply(o_ref[...], _weights(g_ref[first + 1]))
        o_ref[...] = (y.reshape(n_blocks, BLOCK, -1) * table[None]).reshape(y.shape)
        for a in range(n_blocks):
            t_ref[pl.ds(a * BLOCK, BLOCK), :] = o_ref[pl.ds(a * BLOCK, BLOCK), :].T
        t_ref[...] = _apply(t_ref[...], _weights(g_ref[first + 2]))
        for a in range(n_blocks):
            o_ref[pl.ds(a * BLOCK, BLOCK), :] = t_ref[pl.ds(a * BLOCK, BLOCK), :].T


def layers(x, gate_stack, coupling, gate_base, cpl_base, cycles):
    kernel = functools.partial(_layers_kernel, gate_base=gate_base, cpl_base=cpl_base, cycles=cycles)
    return pl.pallas_call(
        kernel,
        out_shape=jax.ShapeDtypeStruct(x.shape, x.dtype),
        scratch_shapes=[pltpu.VMEM(x.shape, jnp.float32)],
    )(x, gate_stack, coupling)


HIGHEST_PREC = lax.Precision.HIGHEST


def partner(value, axis, distance):
    mask = 2**distance
    pairs = [(source, source ^ mask) for source in range(lax.axis_size(axis))]
    return lax.ppermute(value, axis, pairs)


def effective(weight_mat):
    order_size = weight_mat.shape[0]
    return 0.9 * jnp.eye(order_size, dtype=weight_mat.dtype) + 0.45 * weight_mat


def apply_lane(tensor, weight_mat):
    return jnp.dot(tensor, effective(weight_mat), precision=HIGHEST_PREC)


def apply_mid(tensor, weight_mat):
    order_size = weight_mat.shape[0]
    shaped = tensor.reshape(-1, order_size, tensor.shape[1])
    mixed = jnp.einsum("aic,ij->ajc", shaped, effective(weight_mat), precision=HIGHEST_PREC)
    return mixed.reshape(tensor.shape)


def apply_top(tensor, weight_mat):
    order_size = weight_mat.shape[0]
    shaped = tensor.reshape(order_size, -1)
    mixed = jnp.dot(effective(weight_mat).T, shaped, precision=HIGHEST_PREC)
    return mixed.reshape(tensor.shape)


def apply_couple(tensor, table):
    shaped = tensor.reshape(-1, table.shape[0], tensor.shape[1])
    return (shaped * table[None]).reshape(tensor.shape)


def layer_group(tensor, gate_stack, coupling, gate_base, cpl_base, cycles):
    for turn_index in range(cycles):
        first = gate_base + 3 * turn_index
        tensor = apply_top(tensor, gate_stack[first])
        tensor = apply_lane(tensor, gate_stack[first + 1])
        tensor = apply_couple(tensor, coupling[cpl_base + turn_index])
        tensor = apply_mid(tensor, gate_stack[first + 2])
    return tensor


def final_group_cols(cols, gate_stack, coupling, col_start):
    order_size = gate_stack.shape[1]
    width = cols.shape[0]
    gate_base = 3 * CYC_A + 3 * CYC_B
    cpl_base = CYC_A + CYC_B
    for turn_index in range(CYC_C):
        top_mat = effective(gate_stack[gate_base + 2 * turn_index])
        shaped = cols.reshape(width, order_size, -1)
        cols = jnp.einsum("cit,ij->cjt", shaped, top_mat, precision=HIGHEST_PREC).reshape(cols.shape)
        table = lax.dynamic_slice_in_dim(coupling[cpl_base + turn_index], col_start, width, axis=1)
        shaped = cols.reshape(width, -1, order_size)
        cols = (shaped * table.T[:, None, :]).reshape(cols.shape)
        mid_mat = effective(gate_stack[gate_base + 2 * turn_index + 1])
        cols = jnp.dot(cols.reshape(-1, order_size), mid_mat, precision=HIGHEST_PREC).reshape(cols.shape)
    return cols


def swap_bit(tensor, bit_pos):
    half_rows = tensor.shape[0] // 2
    lower = tensor[:half_rows]
    upper = tensor[half_rows:]
    parity = lax.axis_index(BITS) >> bit_pos & 1
    outgoing = jnp.where(parity == 0, upper, lower)
    incoming = partner(outgoing, BITS, bit_pos)
    return jnp.where(
        parity == 0, jnp.concatenate([lower, incoming], 0), jnp.concatenate([incoming, upper], 0)
    )


def reduce_columns(tensor):
    cols = tensor.T
    for axis in ("x", "yl"):
        n = lax.axis_size(axis)
        blocks = cols.reshape(n, cols.shape[0] // n, cols.shape[1])
        cols = lax.all_to_all(blocks, axis, 0, 0, tiled=False).sum(0)
    return cols


def on_device(boundary, gate_stack, coupling):
    tensor = boundary[0]
    top_bit = lax.axis_size(BITS).bit_length() - 2
    tensor = layers(tensor, gate_stack, coupling, 0, 0, CYC_A)
    tensor = swap_bit(tensor, top_bit)
    tensor = layers(tensor, gate_stack, coupling, 3 * CYC_A, CYC_A, CYC_B)
    cols = reduce_columns(tensor)
    cols = swap_bit(cols.T, 0).T
    col_start = lax.axis_index(CUTS) * cols.shape[0]
    cols = final_group_cols(cols, gate_stack, coupling, col_start)
    return cols.T


def solution(mesh):
    n_bits, n_cuts = mesh.shape["bits"], mesh.shape["cuts"]
    fine = Mesh(mesh.devices.reshape(2, n_bits // 4, 2, n_cuts // 4, 4), BITS + CUTS)
    in_specs = (P(CUTS, BITS, None), P(), P())
    out_specs = P(BITS, CUTS)
    return jax.shard_map(
        on_device, mesh=fine, in_specs=in_specs, out_specs=out_specs, check_vma=False
    )
```

```python
import functools

import jax
import jax.numpy as jnp
from jax import lax
from jax.experimental import pallas as pl
from jax.experimental.pallas import tpu as pltpu
from jax.sharding import Mesh, PartitionSpec as P

CYC_A = 4
CYC_B = 4
CYC_C = 5
BITS = ("yh", "z", "core")
CUTS = ("x", "yl")

BLOCK = 128


def _split(a):
    hi = a.astype(jnp.bfloat16)
    lo = (a - hi.astype(jnp.float32)).astype(jnp.bfloat16)
    return hi, lo


def _weights(g):
    hi, lo = _split(0.45 * g)
    return jnp.concatenate([hi, hi, lo], axis=0)


def _apply(x, w):
    hi, lo = _split(x)
    lhs = jnp.concatenate([hi, lo, hi], axis=1)
    return 0.9 * x + jnp.dot(lhs, w, preferred_element_type=jnp.float32)


def _layers_kernel(x_ref, g_ref, c_ref, o_ref, t_ref, *, gate_base, cpl_base, cycles):
    rows = x_ref.shape[0]
    n_blocks = rows // BLOCK
    o_ref[...] = x_ref[...]
    for turn in range(cycles):
        first = gate_base + 3 * turn
        table = c_ref[cpl_base + turn]
        for t in range(n_blocks):
            t_ref[pl.ds(t * BLOCK, BLOCK), :] = o_ref[pl.ds(t, BLOCK, stride=n_blocks), :].T
        t_ref[...] = _apply(t_ref[...], _weights(g_ref[first]))
        for t in range(n_blocks):
            o_ref[pl.ds(t, BLOCK, stride=n_blocks), :] = t_ref[pl.ds(t * BLOCK, BLOCK), :].T
        y = _apply(o_ref[...], _weights(g_ref[first + 1]))
        o_ref[...] = (y.reshape(n_blocks, BLOCK, -1) * table[None]).reshape(y.shape)
        for a in range(n_blocks):
            t_ref[pl.ds(a * BLOCK, BLOCK), :] = o_ref[pl.ds(a * BLOCK, BLOCK), :].T
        t_ref[...] = _apply(t_ref[...], _weights(g_ref[first + 2]))
        for a in range(n_blocks):
            o_ref[pl.ds(a * BLOCK, BLOCK), :] = t_ref[pl.ds(a * BLOCK, BLOCK), :].T


def layers(x, gate_stack, coupling, gate_base, cpl_base, cycles):
    kernel = functools.partial(_layers_kernel, gate_base=gate_base, cpl_base=cpl_base, cycles=cycles)
    return pl.pallas_call(
        kernel,
        out_shape=jax.ShapeDtypeStruct(x.shape, x.dtype),
        scratch_shapes=[pltpu.VMEM(x.shape, jnp.float32)],
    )(x, gate_stack, coupling)


def _final_kernel(d_ref, g_ref, tab_ref, o_ref, m_ref, *, gate_base, cycles):
    width = d_ref.shape[0]
    n_blocks = d_ref.shape[1] // BLOCK
    for a in range(n_blocks):
        o_ref[pl.ds(a * BLOCK, BLOCK), :] = d_ref[:, pl.ds(a * BLOCK, BLOCK)].T
    for turn in range(cycles):
        for t in range(n_blocks):
            m_ref[pl.ds(t * width, width), :] = o_ref[pl.ds(t, BLOCK, stride=n_blocks), :].T
        m_ref[...] = _apply(m_ref[...], _weights(g_ref[gate_base + 2 * turn]))
        for t in range(n_blocks):
            o_ref[pl.ds(t, BLOCK, stride=n_blocks), :] = m_ref[pl.ds(t * width, width), :].T
        table = tab_ref[turn]
        for a in range(n_blocks):
            m_ref[pl.ds(a * width, width), :] = o_ref[pl.ds(a * BLOCK, BLOCK), :].T * table
        m_ref[...] = _apply(m_ref[...], _weights(g_ref[gate_base + 2 * turn + 1]))
        for a in range(n_blocks):
            o_ref[pl.ds(a * BLOCK, BLOCK), :] = m_ref[pl.ds(a * width, width), :].T


def final_layers(d, gate_stack, tables, gate_base, cycles):
    width, rows = d.shape
    kernel = functools.partial(_final_kernel, gate_base=gate_base, cycles=cycles)
    return pl.pallas_call(
        kernel,
        out_shape=jax.ShapeDtypeStruct((rows, width), d.dtype),
        scratch_shapes=[pltpu.VMEM((BLOCK, BLOCK), jnp.float32)],
    )(d, gate_stack, tables)


HIGHEST_PREC = lax.Precision.HIGHEST


def partner(value, axis, distance):
    mask = 2**distance
    pairs = [(source, source ^ mask) for source in range(lax.axis_size(axis))]
    return lax.ppermute(value, axis, pairs)


def effective(weight_mat):
    order_size = weight_mat.shape[0]
    return 0.9 * jnp.eye(order_size, dtype=weight_mat.dtype) + 0.45 * weight_mat


def apply_lane(tensor, weight_mat):
    return jnp.dot(tensor, effective(weight_mat), precision=HIGHEST_PREC)


def apply_mid(tensor, weight_mat):
    order_size = weight_mat.shape[0]
    shaped = tensor.reshape(-1, order_size, tensor.shape[1])
    mixed = jnp.einsum("aic,ij->ajc", shaped, effective(weight_mat), precision=HIGHEST_PREC)
    return mixed.reshape(tensor.shape)


def apply_top(tensor, weight_mat):
    order_size = weight_mat.shape[0]
    shaped = tensor.reshape(order_size, -1)
    mixed = jnp.dot(effective(weight_mat).T, shaped, precision=HIGHEST_PREC)
    return mixed.reshape(tensor.shape)


def apply_couple(tensor, table):
    shaped = tensor.reshape(-1, table.shape[0], tensor.shape[1])
    return (shaped * table[None]).reshape(tensor.shape)


def layer_group(tensor, gate_stack, coupling, gate_base, cpl_base, cycles):
    for turn_index in range(cycles):
        first = gate_base + 3 * turn_index
        tensor = apply_top(tensor, gate_stack[first])
        tensor = apply_lane(tensor, gate_stack[first + 1])
        tensor = apply_couple(tensor, coupling[cpl_base + turn_index])
        tensor = apply_mid(tensor, gate_stack[first + 2])
    return tensor


def final_group_cols(cols, gate_stack, coupling, col_start):
    order_size = gate_stack.shape[1]
    width = cols.shape[0]
    gate_base = 3 * CYC_A + 3 * CYC_B
    cpl_base = CYC_A + CYC_B
    for turn_index in range(CYC_C):
        top_mat = effective(gate_stack[gate_base + 2 * turn_index])
        shaped = cols.reshape(width, order_size, -1)
        cols = jnp.einsum("cit,ij->cjt", shaped, top_mat, precision=HIGHEST_PREC).reshape(cols.shape)
        table = lax.dynamic_slice_in_dim(coupling[cpl_base + turn_index], col_start, width, axis=1)
        shaped = cols.reshape(width, -1, order_size)
        cols = (shaped * table.T[:, None, :]).reshape(cols.shape)
        mid_mat = effective(gate_stack[gate_base + 2 * turn_index + 1])
        cols = jnp.dot(cols.reshape(-1, order_size), mid_mat, precision=HIGHEST_PREC).reshape(cols.shape)
    return cols


def swap_bit(tensor, bit_pos):
    half_rows = tensor.shape[0] // 2
    lower = tensor[:half_rows]
    upper = tensor[half_rows:]
    parity = lax.axis_index(BITS) >> bit_pos & 1
    outgoing = jnp.where(parity == 0, upper, lower)
    incoming = partner(outgoing, BITS, bit_pos)
    return jnp.where(
        parity == 0, jnp.concatenate([lower, incoming], 0), jnp.concatenate([incoming, upper], 0)
    )


def reduce_columns(tensor):
    cols = tensor.T
    for axis in ("x", "yl"):
        n = lax.axis_size(axis)
        blocks = cols.reshape(n, cols.shape[0] // n, cols.shape[1])
        cols = lax.all_to_all(blocks, axis, 0, 0, tiled=False).sum(0)
    return cols


def on_device(boundary, gate_stack, coupling):
    tensor = boundary[0]
    top_bit = lax.axis_size(BITS).bit_length() - 2
    tensor = layers(tensor, gate_stack, coupling, 0, 0, CYC_A)
    tensor = swap_bit(tensor, top_bit)
    tensor = layers(tensor, gate_stack, coupling, 3 * CYC_A, CYC_A, CYC_B)
    cols = reduce_columns(tensor)
    cols = swap_bit(cols.T, 0).T
    width = cols.shape[0]
    col_start = lax.axis_index(CUTS) * width
    cpl_base = CYC_A + CYC_B
    tables = lax.dynamic_slice_in_dim(coupling[cpl_base:cpl_base + CYC_C], col_start, width, axis=2)
    return final_layers(cols, gate_stack, jnp.swapaxes(tables, 1, 2), 3 * CYC_A + 3 * CYC_B, CYC_C)


def solution(mesh):
    n_bits, n_cuts = mesh.shape["bits"], mesh.shape["cuts"]
    fine = Mesh(mesh.devices.reshape(2, n_bits // 4, 2, n_cuts // 4, 4), BITS + CUTS)
    in_specs = (P(CUTS, BITS, None), P(), P())
    out_specs = P(BITS, CUTS)
    return jax.shard_map(
        on_device, mesh=fine, in_specs=in_specs, out_specs=out_specs, check_vma=False
    )
```

```python
import functools

import jax
import jax.numpy as jnp
from jax import lax
from jax.experimental import pallas as pl
from jax.experimental.pallas import tpu as pltpu
from jax.sharding import Mesh, PartitionSpec as P

CYC_A = 4
CYC_B = 4
CYC_C = 5
BITS = ("yh", "z", "core")
CUTS = ("x", "yl")

BLOCK = 128


def _split(a):
    hi = a.astype(jnp.bfloat16)
    lo = (a - hi.astype(jnp.float32)).astype(jnp.bfloat16)
    return hi, lo


def _weights(g):
    hi, lo = _split(0.45 * g)
    return jnp.concatenate([hi, hi, lo], axis=0)


def _apply(x, w):
    hi, lo = _split(x)
    lhs = jnp.concatenate([hi, lo, hi], axis=1)
    return 0.9 * x + jnp.dot(lhs, w, preferred_element_type=jnp.float32)


def _layer_turns(o_ref, t_ref, g_ref, c_ref, gate_base, cpl_base, cycles, last_to=None):
    rows = o_ref.shape[0]
    n_blocks = rows // BLOCK
    for turn in range(cycles):
        first = gate_base + 3 * turn
        table = c_ref[cpl_base + turn]
        for t in range(n_blocks):
            t_ref[pl.ds(t * BLOCK, BLOCK), :] = o_ref[pl.ds(t, BLOCK, stride=n_blocks), :].T
        t_ref[...] = _apply(t_ref[...], _weights(g_ref[first]))
        for t in range(n_blocks):
            o_ref[pl.ds(t, BLOCK, stride=n_blocks), :] = t_ref[pl.ds(t * BLOCK, BLOCK), :].T
        y = _apply(o_ref[...], _weights(g_ref[first + 1]))
        o_ref[...] = (y.reshape(n_blocks, BLOCK, -1) * table[None]).reshape(y.shape)
        for a in range(n_blocks):
            t_ref[pl.ds(a * BLOCK, BLOCK), :] = o_ref[pl.ds(a * BLOCK, BLOCK), :].T
        t_ref[...] = _apply(t_ref[...], _weights(g_ref[first + 2]))
        if last_to is not None and turn == cycles - 1:
            for a in range(n_blocks):
                last_to[:, pl.ds(a * BLOCK, BLOCK)] = t_ref[pl.ds(a * BLOCK, BLOCK), :]
        else:
            for a in range(n_blocks):
                o_ref[pl.ds(a * BLOCK, BLOCK), :] = t_ref[pl.ds(a * BLOCK, BLOCK), :].T


def _group_a_kernel(p_ref, x_ref, g_ref, c_ref, keep_ref, send_ref, o_ref, t_ref, *, cycles):
    half = keep_ref.shape[0]
    o_ref[...] = x_ref[...]
    _layer_turns(o_ref, t_ref, g_ref, c_ref, 0, 0, cycles)
    p = p_ref[0]
    keep_ref[...] = o_ref[pl.ds(pl.multiple_of(p * half, half), half), :]
    send_ref[...] = o_ref[pl.ds(pl.multiple_of((1 - p) * half, half), half), :]


def _group_b_kernel(p_ref, keep_ref, recv_ref, g_ref, c_ref, out_ref, o_ref, t_ref, *, gate_base, cpl_base, cycles):
    half = keep_ref.shape[0]
    p = p_ref[0]
    o_ref[pl.ds(pl.multiple_of(p * half, half), half), :] = keep_ref[...]
    o_ref[pl.ds(pl.multiple_of((1 - p) * half, half), half), :] = recv_ref[...]
    _layer_turns(o_ref, t_ref, g_ref, c_ref, gate_base, cpl_base, cycles, last_to=out_ref)


def _smem():
    return pl.BlockSpec(memory_space=pltpu.SMEM)


def _vmem():
    return pl.BlockSpec(memory_space=pltpu.VMEM)


def group_a(parity, x, gate_stack, coupling, cycles):
    half = jax.ShapeDtypeStruct((x.shape[0] // 2, x.shape[1]), x.dtype)
    return pl.pallas_call(
        functools.partial(_group_a_kernel, cycles=cycles),
        out_shape=(half, half),
        in_specs=[_smem(), _vmem(), _vmem(), _vmem()],
        out_specs=(_vmem(), _vmem()),
        scratch_shapes=[pltpu.VMEM(x.shape, jnp.float32), pltpu.VMEM(x.shape, jnp.float32)],
    )(parity, x, gate_stack, coupling)


def group_b(parity, keep, recv, gate_stack, coupling, gate_base, cpl_base, cycles):
    rows, cols = keep.shape[0] * 2, keep.shape[1]
    kernel = functools.partial(_group_b_kernel, gate_base=gate_base, cpl_base=cpl_base, cycles=cycles)
    return pl.pallas_call(
        kernel,
        out_shape=jax.ShapeDtypeStruct((cols, rows), keep.dtype),
        in_specs=[_smem(), _vmem(), _vmem(), _vmem(), _vmem()],
        out_specs=_vmem(),
        scratch_shapes=[pltpu.VMEM((rows, cols), jnp.float32), pltpu.VMEM((rows, cols), jnp.float32)],
    )(parity, keep, recv, gate_stack, coupling)


def _final_kernel(d_ref, g_ref, tab_ref, o_ref, m_ref, *, gate_base, cycles):
    width = d_ref.shape[0]
    n_blocks = d_ref.shape[1] // BLOCK
    for a in range(n_blocks):
        o_ref[pl.ds(a * BLOCK, BLOCK), :] = d_ref[:, pl.ds(a * BLOCK, BLOCK)].T
    for turn in range(cycles):
        for t in range(n_blocks):
            m_ref[pl.ds(t * width, width), :] = o_ref[pl.ds(t, BLOCK, stride=n_blocks), :].T
        m_ref[...] = _apply(m_ref[...], _weights(g_ref[gate_base + 2 * turn]))
        for t in range(n_blocks):
            o_ref[pl.ds(t, BLOCK, stride=n_blocks), :] = m_ref[pl.ds(t * width, width), :].T
        table = tab_ref[turn]
        for a in range(n_blocks):
            m_ref[pl.ds(a * width, width), :] = o_ref[pl.ds(a * BLOCK, BLOCK), :].T * table
        m_ref[...] = _apply(m_ref[...], _weights(g_ref[gate_base + 2 * turn + 1]))
        for a in range(n_blocks):
            o_ref[pl.ds(a * BLOCK, BLOCK), :] = m_ref[pl.ds(a * width, width), :].T


def final_layers(d, gate_stack, tables, gate_base, cycles):
    width, rows = d.shape
    kernel = functools.partial(_final_kernel, gate_base=gate_base, cycles=cycles)
    return pl.pallas_call(
        kernel,
        out_shape=jax.ShapeDtypeStruct((rows, width), d.dtype),
        scratch_shapes=[pltpu.VMEM((BLOCK, BLOCK), jnp.float32)],
    )(d, gate_stack, tables)


HIGHEST_PREC = lax.Precision.HIGHEST


def partner(value, axis, distance):
    mask = 2**distance
    pairs = [(source, source ^ mask) for source in range(lax.axis_size(axis))]
    return lax.ppermute(value, axis, pairs)


def effective(weight_mat):
    order_size = weight_mat.shape[0]
    return 0.9 * jnp.eye(order_size, dtype=weight_mat.dtype) + 0.45 * weight_mat


def apply_lane(tensor, weight_mat):
    return jnp.dot(tensor, effective(weight_mat), precision=HIGHEST_PREC)


def apply_mid(tensor, weight_mat):
    order_size = weight_mat.shape[0]
    shaped = tensor.reshape(-1, order_size, tensor.shape[1])
    mixed = jnp.einsum("aic,ij->ajc", shaped, effective(weight_mat), precision=HIGHEST_PREC)
    return mixed.reshape(tensor.shape)


def apply_top(tensor, weight_mat):
    order_size = weight_mat.shape[0]
    shaped = tensor.reshape(order_size, -1)
    mixed = jnp.dot(effective(weight_mat).T, shaped, precision=HIGHEST_PREC)
    return mixed.reshape(tensor.shape)


def apply_couple(tensor, table):
    shaped = tensor.reshape(-1, table.shape[0], tensor.shape[1])
    return (shaped * table[None]).reshape(tensor.shape)


def layer_group(tensor, gate_stack, coupling, gate_base, cpl_base, cycles):
    for turn_index in range(cycles):
        first = gate_base + 3 * turn_index
        tensor = apply_top(tensor, gate_stack[first])
        tensor = apply_lane(tensor, gate_stack[first + 1])
        tensor = apply_couple(tensor, coupling[cpl_base + turn_index])
        tensor = apply_mid(tensor, gate_stack[first + 2])
    return tensor


def final_group_cols(cols, gate_stack, coupling, col_start):
    order_size = gate_stack.shape[1]
    width = cols.shape[0]
    gate_base = 3 * CYC_A + 3 * CYC_B
    cpl_base = CYC_A + CYC_B
    for turn_index in range(CYC_C):
        top_mat = effective(gate_stack[gate_base + 2 * turn_index])
        shaped = cols.reshape(width, order_size, -1)
        cols = jnp.einsum("cit,ij->cjt", shaped, top_mat, precision=HIGHEST_PREC).reshape(cols.shape)
        table = lax.dynamic_slice_in_dim(coupling[cpl_base + turn_index], col_start, width, axis=1)
        shaped = cols.reshape(width, -1, order_size)
        cols = (shaped * table.T[:, None, :]).reshape(cols.shape)
        mid_mat = effective(gate_stack[gate_base + 2 * turn_index + 1])
        cols = jnp.dot(cols.reshape(-1, order_size), mid_mat, precision=HIGHEST_PREC).reshape(cols.shape)
    return cols


def swap_bit(tensor, bit_pos):
    half_rows = tensor.shape[0] // 2
    lower = tensor[:half_rows]
    upper = tensor[half_rows:]
    parity = lax.axis_index(BITS) >> bit_pos & 1
    outgoing = jnp.where(parity == 0, upper, lower)
    incoming = partner(outgoing, BITS, bit_pos)
    return jnp.where(
        parity == 0, jnp.concatenate([lower, incoming], 0), jnp.concatenate([incoming, upper], 0)
    )


def reduce_columns(cols):
    for axis in ("x", "yl"):
        n = lax.axis_size(axis)
        blocks = cols.reshape(n, cols.shape[0] // n, cols.shape[1])
        cols = lax.all_to_all(blocks, axis, 0, 0, tiled=False).sum(0)
    return cols


def swap_lanes(cols, bit_pos):
    half = cols.shape[1] // 2
    lower = cols[:, :half]
    upper = cols[:, half:]
    parity = lax.axis_index(BITS) >> bit_pos & 1
    outgoing = jnp.where(parity == 0, upper, lower)
    incoming = partner(outgoing, BITS, bit_pos)
    return jnp.where(
        parity == 0, jnp.concatenate([lower, incoming], 1), jnp.concatenate([incoming, upper], 1)
    )


def on_device(boundary, gate_stack, coupling):
    top_bit = lax.axis_size(BITS).bit_length() - 2
    parity = (lax.axis_index(BITS) >> top_bit & 1).astype(jnp.int32).reshape(1)
    keep, send = group_a(parity, boundary[0], gate_stack, coupling, CYC_A)
    recv = partner(send, BITS, top_bit)
    cols = group_b(parity, keep, recv, gate_stack, coupling, 3 * CYC_A, CYC_A, CYC_B)
    cols = swap_lanes(reduce_columns(cols), 0)
    width = cols.shape[0]
    col_start = lax.axis_index(CUTS) * width
    cpl_base = CYC_A + CYC_B
    tables = lax.dynamic_slice_in_dim(coupling[cpl_base:cpl_base + CYC_C], col_start, width, axis=2)
    return final_layers(cols, gate_stack, jnp.swapaxes(tables, 1, 2), 3 * CYC_A + 3 * CYC_B, CYC_C)


def solution(mesh):
    n_bits, n_cuts = mesh.shape["bits"], mesh.shape["cuts"]
    fine = Mesh(mesh.devices.reshape(2, n_bits // 4, 2, n_cuts // 4, 4), BITS + CUTS)
    in_specs = (P(CUTS, BITS, None), P(), P())
    out_specs = P(BITS, CUTS)
    return jax.shard_map(
        on_device, mesh=fine, in_specs=in_specs, out_specs=out_specs, check_vma=False
    )
```

```python
import functools

import jax
import jax.numpy as jnp
from jax import lax
from jax.experimental import pallas as pl
from jax.experimental.pallas import tpu as pltpu
from jax.sharding import Mesh, PartitionSpec as P

CYC_A = 4
CYC_B = 4
CYC_C = 5
BITS = ("yh", "z", "core")
CUTS = ("x", "yl")

BLOCK = 128


def _split(a):
    hi = a.astype(jnp.bfloat16)
    lo = (a - hi.astype(jnp.float32)).astype(jnp.bfloat16)
    return hi, lo


def _weights(g):
    hi, lo = _split(0.45 * g)
    return jnp.concatenate([hi, hi, lo], axis=0)


def _apply(x, w):
    hi, lo = _split(x)
    lhs = jnp.concatenate([hi, lo, hi], axis=1)
    return 0.9 * x + jnp.dot(lhs, w, preferred_element_type=jnp.float32)


def _layer_turns(o_ref, t_ref, g_ref, c_ref, gate_base, cpl_base, cycles, last_to=None):
    rows = o_ref.shape[0]
    n_blocks = rows // BLOCK
    for turn in range(cycles):
        first = gate_base + 3 * turn
        table = c_ref[cpl_base + turn]
        for t in range(n_blocks):
            t_ref[pl.ds(t * BLOCK, BLOCK), :] = o_ref[pl.ds(t, BLOCK, stride=n_blocks), :].T
        t_ref[...] = _apply(t_ref[...], _weights(g_ref[first]))
        for t in range(n_blocks):
            o_ref[pl.ds(t, BLOCK, stride=n_blocks), :] = t_ref[pl.ds(t * BLOCK, BLOCK), :].T
        y = _apply(o_ref[...], _weights(g_ref[first + 1]))
        o_ref[...] = (y.reshape(n_blocks, BLOCK, -1) * table[None]).reshape(y.shape)
        for a in range(n_blocks):
            t_ref[pl.ds(a * BLOCK, BLOCK), :] = o_ref[pl.ds(a * BLOCK, BLOCK), :].T
        t_ref[...] = _apply(t_ref[...], _weights(g_ref[first + 2]))
        if last_to is not None and turn == cycles - 1:
            for a in range(n_blocks):
                last_to[:, pl.ds(a * BLOCK, BLOCK)] = t_ref[pl.ds(a * BLOCK, BLOCK), :]
        else:
            for a in range(n_blocks):
                o_ref[pl.ds(a * BLOCK, BLOCK), :] = t_ref[pl.ds(a * BLOCK, BLOCK), :].T


def _group_a_kernel(p_ref, x_ref, g_ref, c_ref, keep_ref, send_ref, o_ref, t_ref, *, cycles):
    half = keep_ref.shape[0]
    o_ref[...] = x_ref[...]
    _layer_turns(o_ref, t_ref, g_ref, c_ref, 0, 0, cycles)
    p = p_ref[0]
    keep_ref[...] = o_ref[pl.ds(pl.multiple_of(p * half, half), half), :]
    send_ref[...] = o_ref[pl.ds(pl.multiple_of((1 - p) * half, half), half), :]


def _group_b_kernel(p_ref, keep_ref, recv_ref, g_ref, c_ref, out_ref, o_ref, t_ref, *, gate_base, cpl_base, cycles):
    half = keep_ref.shape[0]
    p = p_ref[0]
    o_ref[pl.ds(pl.multiple_of(p * half, half), half), :] = keep_ref[...]
    o_ref[pl.ds(pl.multiple_of((1 - p) * half, half), half), :] = recv_ref[...]
    _layer_turns(o_ref, t_ref, g_ref, c_ref, gate_base, cpl_base, cycles, last_to=out_ref)


def _smem():
    return pl.BlockSpec(memory_space=pltpu.SMEM)


def _vmem():
    return pl.BlockSpec(memory_space=pltpu.VMEM)


def group_a(parity, x, gate_stack, coupling, cycles):
    half = jax.ShapeDtypeStruct((x.shape[0] // 2, x.shape[1]), x.dtype)
    return pl.pallas_call(
        functools.partial(_group_a_kernel, cycles=cycles),
        out_shape=(half, half),
        in_specs=[_smem(), _vmem(), _vmem(), _vmem()],
        out_specs=(_vmem(), _vmem()),
        scratch_shapes=[pltpu.VMEM(x.shape, jnp.float32), pltpu.VMEM(x.shape, jnp.float32)],
    )(parity, x, gate_stack, coupling)


def group_b(parity, keep, recv, gate_stack, coupling, gate_base, cpl_base, cycles):
    rows, cols = keep.shape[0] * 2, keep.shape[1]
    kernel = functools.partial(_group_b_kernel, gate_base=gate_base, cpl_base=cpl_base, cycles=cycles)
    return pl.pallas_call(
        kernel,
        out_shape=jax.ShapeDtypeStruct((cols, rows), keep.dtype),
        in_specs=[_smem(), _vmem(), _vmem(), _vmem(), _vmem()],
        out_specs=_vmem(),
        scratch_shapes=[pltpu.VMEM((rows, cols), jnp.float32), pltpu.VMEM((rows, cols), jnp.float32)],
    )(parity, keep, recv, gate_stack, coupling)


def _final_kernel(d_ref, g_ref, tab_ref, out_ref, o_ref, m_ref, *, gate_base, cycles):
    width = d_ref.shape[0]
    n_blocks = d_ref.shape[1] // BLOCK
    for a in range(n_blocks):
        o_ref[pl.ds(a * BLOCK, BLOCK), :] = d_ref[:, pl.ds(a * BLOCK, BLOCK)].T
    for turn in range(cycles):
        for t in range(n_blocks):
            m_ref[pl.ds(t * width, width), :] = o_ref[pl.ds(t, BLOCK, stride=n_blocks), :].T
        m_ref[...] = _apply(m_ref[...], _weights(g_ref[gate_base + 2 * turn]))
        for t in range(n_blocks):
            o_ref[pl.ds(t, BLOCK, stride=n_blocks), :] = m_ref[pl.ds(t * width, width), :].T
        table = tab_ref[turn]
        for a in range(n_blocks):
            m_ref[pl.ds(a * width, width), :] = o_ref[pl.ds(a * BLOCK, BLOCK), :].T * table
        m_ref[...] = _apply(m_ref[...], _weights(g_ref[gate_base + 2 * turn + 1]))
        for a in range(n_blocks):
            if turn == cycles - 1:
                out_ref[:, pl.ds(a * BLOCK, BLOCK)] = m_ref[pl.ds(a * width, width), :]
            else:
                o_ref[pl.ds(a * BLOCK, BLOCK), :] = m_ref[pl.ds(a * width, width), :].T


def final_layers(d, gate_stack, tables, gate_base, cycles):
    width, rows = d.shape
    kernel = functools.partial(_final_kernel, gate_base=gate_base, cycles=cycles)
    out = pl.pallas_call(
        kernel,
        out_shape=jax.ShapeDtypeStruct((width, rows), d.dtype),
        scratch_shapes=[pltpu.VMEM((rows, width), jnp.float32), pltpu.VMEM((BLOCK, BLOCK), jnp.float32)],
    )(d, gate_stack, tables)
    return out.T


HIGHEST_PREC = lax.Precision.HIGHEST


def partner(value, axis, distance):
    mask = 2**distance
    pairs = [(source, source ^ mask) for source in range(lax.axis_size(axis))]
    return lax.ppermute(value, axis, pairs)


def effective(weight_mat):
    order_size = weight_mat.shape[0]
    return 0.9 * jnp.eye(order_size, dtype=weight_mat.dtype) + 0.45 * weight_mat


def apply_lane(tensor, weight_mat):
    return jnp.dot(tensor, effective(weight_mat), precision=HIGHEST_PREC)


def apply_mid(tensor, weight_mat):
    order_size = weight_mat.shape[0]
    shaped = tensor.reshape(-1, order_size, tensor.shape[1])
    mixed = jnp.einsum("aic,ij->ajc", shaped, effective(weight_mat), precision=HIGHEST_PREC)
    return mixed.reshape(tensor.shape)


def apply_top(tensor, weight_mat):
    order_size = weight_mat.shape[0]
    shaped = tensor.reshape(order_size, -1)
    mixed = jnp.dot(effective(weight_mat).T, shaped, precision=HIGHEST_PREC)
    return mixed.reshape(tensor.shape)


def apply_couple(tensor, table):
    shaped = tensor.reshape(-1, table.shape[0], tensor.shape[1])
    return (shaped * table[None]).reshape(tensor.shape)


def layer_group(tensor, gate_stack, coupling, gate_base, cpl_base, cycles):
    for turn_index in range(cycles):
        first = gate_base + 3 * turn_index
        tensor = apply_top(tensor, gate_stack[first])
        tensor = apply_lane(tensor, gate_stack[first + 1])
        tensor = apply_couple(tensor, coupling[cpl_base + turn_index])
        tensor = apply_mid(tensor, gate_stack[first + 2])
    return tensor


def final_group_cols(cols, gate_stack, coupling, col_start):
    order_size = gate_stack.shape[1]
    width = cols.shape[0]
    gate_base = 3 * CYC_A + 3 * CYC_B
    cpl_base = CYC_A + CYC_B
    for turn_index in range(CYC_C):
        top_mat = effective(gate_stack[gate_base + 2 * turn_index])
        shaped = cols.reshape(width, order_size, -1)
        cols = jnp.einsum("cit,ij->cjt", shaped, top_mat, precision=HIGHEST_PREC).reshape(cols.shape)
        table = lax.dynamic_slice_in_dim(coupling[cpl_base + turn_index], col_start, width, axis=1)
        shaped = cols.reshape(width, -1, order_size)
        cols = (shaped * table.T[:, None, :]).reshape(cols.shape)
        mid_mat = effective(gate_stack[gate_base + 2 * turn_index + 1])
        cols = jnp.dot(cols.reshape(-1, order_size), mid_mat, precision=HIGHEST_PREC).reshape(cols.shape)
    return cols


def swap_bit(tensor, bit_pos):
    half_rows = tensor.shape[0] // 2
    lower = tensor[:half_rows]
    upper = tensor[half_rows:]
    parity = lax.axis_index(BITS) >> bit_pos & 1
    outgoing = jnp.where(parity == 0, upper, lower)
    incoming = partner(outgoing, BITS, bit_pos)
    return jnp.where(
        parity == 0, jnp.concatenate([lower, incoming], 0), jnp.concatenate([incoming, upper], 0)
    )


def reduce_columns(cols):
    for axis in ("x", "yl"):
        n = lax.axis_size(axis)
        blocks = cols.reshape(n, cols.shape[0] // n, cols.shape[1])
        cols = lax.all_to_all(blocks, axis, 0, 0, tiled=False).sum(0)
    return cols


def swap_lanes(cols, bit_pos):
    half = cols.shape[1] // 2
    lower = cols[:, :half]
    upper = cols[:, half:]
    parity = lax.axis_index(BITS) >> bit_pos & 1
    outgoing = jnp.where(parity == 0, upper, lower)
    incoming = partner(outgoing, BITS, bit_pos)
    return jnp.where(
        parity == 0, jnp.concatenate([lower, incoming], 1), jnp.concatenate([incoming, upper], 1)
    )


def on_device(boundary, gate_stack, coupling):
    top_bit = lax.axis_size(BITS).bit_length() - 2
    parity = (lax.axis_index(BITS) >> top_bit & 1).astype(jnp.int32).reshape(1)
    keep, send = group_a(parity, boundary[0], gate_stack, coupling, CYC_A)
    recv = partner(send, BITS, top_bit)
    cols = group_b(parity, keep, recv, gate_stack, coupling, 3 * CYC_A, CYC_A, CYC_B)
    cols = swap_lanes(reduce_columns(cols), 0)
    width = cols.shape[0]
    col_start = lax.axis_index(CUTS) * width
    cpl_base = CYC_A + CYC_B
    tables = lax.dynamic_slice_in_dim(coupling[cpl_base:cpl_base + CYC_C], col_start, width, axis=2)
    return final_layers(cols, gate_stack, jnp.swapaxes(tables, 1, 2), 3 * CYC_A + 3 * CYC_B, CYC_C)


def solution(mesh):
    n_bits, n_cuts = mesh.shape["bits"], mesh.shape["cuts"]
    fine = Mesh(mesh.devices.reshape(2, n_bits // 4, 2, n_cuts // 4, 4), BITS + CUTS)
    in_specs = (P(CUTS, BITS, None), P(), P())
    out_specs = P(BITS, CUTS)
    return jax.shard_map(
        on_device, mesh=fine, in_specs=in_specs, out_specs=out_specs, check_vma=False
    )
```

```python
import functools

import jax
import jax.numpy as jnp
from jax import lax
from jax.experimental import pallas as pl
from jax.experimental.pallas import tpu as pltpu
from jax.sharding import Mesh, PartitionSpec as P

CYC_A = 4
CYC_B = 4
CYC_C = 5
BITS = ("yh", "z", "core")
CUTS = ("x", "yl")

BLOCK = 128


def _split(a):
    hi = a.astype(jnp.bfloat16)
    lo = (a - hi.astype(jnp.float32)).astype(jnp.bfloat16)
    return hi, lo


def _weights(g):
    hi, lo = _split(0.45 * g)
    return jnp.concatenate([hi, hi, lo], axis=0)


def _apply(x, w):
    hi, lo = _split(x)
    lhs = jnp.concatenate([hi, lo, hi], axis=1)
    return 0.9 * x + jnp.dot(lhs, w, preferred_element_type=jnp.float32)


def _weights_left(g):
    hi, lo = _split((0.45 * g).T)
    return jnp.concatenate([hi, lo, hi], axis=1)


def _apply_left(w, x):
    hi, lo = _split(x)
    rhs = jnp.concatenate([hi, hi, lo], axis=0)
    return 0.9 * x + jnp.dot(w, rhs, preferred_element_type=jnp.float32)


def _layer_turns(o_ref, t_ref, g_ref, c_ref, cycles, last_to=None):
    rows = o_ref.shape[0]
    n_blocks = rows // BLOCK
    for turn in range(cycles):
        first = 3 * turn
        table = c_ref[turn]
        xs = jnp.concatenate([o_ref[pl.ds(t, BLOCK, stride=n_blocks), :] for t in range(n_blocks)], axis=1)
        ys = _apply_left(_weights_left(g_ref[first]), xs)
        for t in range(n_blocks):
            o_ref[pl.ds(t, BLOCK, stride=n_blocks), :] = ys[:, t * BLOCK:(t + 1) * BLOCK]
        y = _apply(o_ref[...], _weights(g_ref[first + 1]))
        o_ref[...] = (y.reshape(n_blocks, BLOCK, -1) * table[None]).reshape(y.shape)
        if last_to is not None and turn == cycles - 1:
            for a in range(n_blocks):
                t_ref[pl.ds(a * BLOCK, BLOCK), :] = o_ref[pl.ds(a * BLOCK, BLOCK), :].T
            t_ref[...] = _apply(t_ref[...], _weights(g_ref[first + 2]))
            for a in range(n_blocks):
                last_to[:, pl.ds(a * BLOCK, BLOCK)] = t_ref[pl.ds(a * BLOCK, BLOCK), :]
        else:
            xs = jnp.concatenate([o_ref[pl.ds(a * BLOCK, BLOCK), :] for a in range(n_blocks)], axis=1)
            ys = _apply_left(_weights_left(g_ref[first + 2]), xs)
            for a in range(n_blocks):
                o_ref[pl.ds(a * BLOCK, BLOCK), :] = ys[:, a * BLOCK:(a + 1) * BLOCK]


def _group_a_kernel(p_ref, x_ref, g_ref, c_ref, keep_ref, send_ref, o_ref, *, cycles):
    half = keep_ref.shape[0]
    o_ref[...] = x_ref[...]
    _layer_turns(o_ref, None, g_ref, c_ref, cycles)
    p = p_ref[0]
    keep_ref[...] = o_ref[pl.ds(pl.multiple_of(p * half, half), half), :]
    send_ref[...] = o_ref[pl.ds(pl.multiple_of((1 - p) * half, half), half), :]


def _group_b_kernel(p_ref, keep_ref, recv_ref, g_ref, c_ref, out_ref, o_ref, t_ref, *, cycles):
    half = keep_ref.shape[0]
    p = p_ref[0]
    o_ref[pl.ds(pl.multiple_of(p * half, half), half), :] = keep_ref[...]
    o_ref[pl.ds(pl.multiple_of((1 - p) * half, half), half), :] = recv_ref[...]
    _layer_turns(o_ref, t_ref, g_ref, c_ref, cycles, last_to=out_ref)


def _smem():
    return pl.BlockSpec(memory_space=pltpu.SMEM)


def _vmem():
    return pl.BlockSpec(memory_space=pltpu.VMEM)


def _stack_block(count, index):
    return pl.BlockSpec((count, BLOCK, BLOCK), lambda step: (index, 0, 0), memory_space=pltpu.VMEM)


def group_a(parity, x, gate_stack, coupling, cycles):
    half = jax.ShapeDtypeStruct((x.shape[0] // 2, x.shape[1]), x.dtype)
    return pl.pallas_call(
        functools.partial(_group_a_kernel, cycles=cycles),
        out_shape=(half, half),
        grid=(1,),
        in_specs=[_smem(), _vmem(), _stack_block(3 * cycles, 0), _stack_block(cycles, 0)],
        out_specs=(_vmem(), _vmem()),
        scratch_shapes=[pltpu.VMEM(x.shape, jnp.float32)],
    )(parity, x, gate_stack, coupling)


def group_b(parity, keep, recv, gate_stack, coupling, cycles):
    rows, cols = keep.shape[0] * 2, keep.shape[1]
    return pl.pallas_call(
        functools.partial(_group_b_kernel, cycles=cycles),
        out_shape=jax.ShapeDtypeStruct((cols, rows), keep.dtype),
        grid=(1,),
        in_specs=[_smem(), _vmem(), _vmem(), _stack_block(3 * cycles, 1), _stack_block(cycles, 1)],
        out_specs=_vmem(),
        scratch_shapes=[pltpu.VMEM((rows, cols), jnp.float32), pltpu.VMEM((rows, cols), jnp.float32)],
    )(parity, keep, recv, gate_stack, coupling)


def _final_kernel(d_ref, g_ref, tab_ref, out_ref, o_ref, m_ref, *, gate_base, cycles):
    width = d_ref.shape[0]
    n_blocks = d_ref.shape[1] // BLOCK
    for a in range(n_blocks):
        o_ref[pl.ds(a * BLOCK, BLOCK), :] = d_ref[:, pl.ds(a * BLOCK, BLOCK)].T
    for turn in range(cycles):
        for t in range(n_blocks):
            m_ref[pl.ds(t * width, width), :] = o_ref[pl.ds(t, BLOCK, stride=n_blocks), :].T
        m_ref[...] = _apply(m_ref[...], _weights(g_ref[gate_base + 2 * turn]))
        for t in range(n_blocks):
            o_ref[pl.ds(t, BLOCK, stride=n_blocks), :] = m_ref[pl.ds(t * width, width), :].T
        table = tab_ref[turn]
        for a in range(n_blocks):
            m_ref[pl.ds(a * width, width), :] = o_ref[pl.ds(a * BLOCK, BLOCK), :].T * table
        m_ref[...] = _apply(m_ref[...], _weights(g_ref[gate_base + 2 * turn + 1]))
        for a in range(n_blocks):
            if turn == cycles - 1:
                out_ref[:, pl.ds(a * BLOCK, BLOCK)] = m_ref[pl.ds(a * width, width), :]
            else:
                o_ref[pl.ds(a * BLOCK, BLOCK), :] = m_ref[pl.ds(a * width, width), :].T


def final_layers(d, gate_stack, tables, gate_base, cycles):
    width, rows = d.shape
    kernel = functools.partial(_final_kernel, gate_base=gate_base, cycles=cycles)
    out = pl.pallas_call(
        kernel,
        out_shape=jax.ShapeDtypeStruct((width, rows), d.dtype),
        scratch_shapes=[pltpu.VMEM((rows, width), jnp.float32), pltpu.VMEM((BLOCK, BLOCK), jnp.float32)],
    )(d, gate_stack, tables)
    return out.T


HIGHEST_PREC = lax.Precision.HIGHEST


def partner(value, axis, distance):
    mask = 2**distance
    pairs = [(source, source ^ mask) for source in range(lax.axis_size(axis))]
    return lax.ppermute(value, axis, pairs)


def effective(weight_mat):
    order_size = weight_mat.shape[0]
    return 0.9 * jnp.eye(order_size, dtype=weight_mat.dtype) + 0.45 * weight_mat


def apply_lane(tensor, weight_mat):
    return jnp.dot(tensor, effective(weight_mat), precision=HIGHEST_PREC)


def apply_mid(tensor, weight_mat):
    order_size = weight_mat.shape[0]
    shaped = tensor.reshape(-1, order_size, tensor.shape[1])
    mixed = jnp.einsum("aic,ij->ajc", shaped, effective(weight_mat), precision=HIGHEST_PREC)
    return mixed.reshape(tensor.shape)


def apply_top(tensor, weight_mat):
    order_size = weight_mat.shape[0]
    shaped = tensor.reshape(order_size, -1)
    mixed = jnp.dot(effective(weight_mat).T, shaped, precision=HIGHEST_PREC)
    return mixed.reshape(tensor.shape)


def apply_couple(tensor, table):
    shaped = tensor.reshape(-1, table.shape[0], tensor.shape[1])
    return (shaped * table[None]).reshape(tensor.shape)


def layer_group(tensor, gate_stack, coupling, gate_base, cpl_base, cycles):
    for turn_index in range(cycles):
        first = gate_base + 3 * turn_index
        tensor = apply_top(tensor, gate_stack[first])
        tensor = apply_lane(tensor, gate_stack[first + 1])
        tensor = apply_couple(tensor, coupling[cpl_base + turn_index])
        tensor = apply_mid(tensor, gate_stack[first + 2])
    return tensor


def final_group_cols(cols, gate_stack, coupling, col_start):
    order_size = gate_stack.shape[1]
    width = cols.shape[0]
    gate_base = 3 * CYC_A + 3 * CYC_B
    cpl_base = CYC_A + CYC_B
    for turn_index in range(CYC_C):
        top_mat = effective(gate_stack[gate_base + 2 * turn_index])
        shaped = cols.reshape(width, order_size, -1)
        cols = jnp.einsum("cit,ij->cjt", shaped, top_mat, precision=HIGHEST_PREC).reshape(cols.shape)
        table = lax.dynamic_slice_in_dim(coupling[cpl_base + turn_index], col_start, width, axis=1)
        shaped = cols.reshape(width, -1, order_size)
        cols = (shaped * table.T[:, None, :]).reshape(cols.shape)
        mid_mat = effective(gate_stack[gate_base + 2 * turn_index + 1])
        cols = jnp.dot(cols.reshape(-1, order_size), mid_mat, precision=HIGHEST_PREC).reshape(cols.shape)
    return cols


def swap_bit(tensor, bit_pos):
    half_rows = tensor.shape[0] // 2
    lower = tensor[:half_rows]
    upper = tensor[half_rows:]
    parity = lax.axis_index(BITS) >> bit_pos & 1
    outgoing = jnp.where(parity == 0, upper, lower)
    incoming = partner(outgoing, BITS, bit_pos)
    return jnp.where(
        parity == 0, jnp.concatenate([lower, incoming], 0), jnp.concatenate([incoming, upper], 0)
    )


def reduce_columns(cols):
    for axis in ("x", "yl"):
        n = lax.axis_size(axis)
        blocks = cols.reshape(n, cols.shape[0] // n, cols.shape[1])
        cols = lax.all_to_all(blocks, axis, 0, 0, tiled=False).sum(0)
    return cols


def swap_lanes(cols, bit_pos):
    half = cols.shape[1] // 2
    lower = cols[:, :half]
    upper = cols[:, half:]
    parity = lax.axis_index(BITS) >> bit_pos & 1
    outgoing = jnp.where(parity == 0, upper, lower)
    incoming = partner(outgoing, BITS, bit_pos)
    return jnp.where(
        parity == 0, jnp.concatenate([lower, incoming], 1), jnp.concatenate([incoming, upper], 1)
    )


def on_device(boundary, gate_stack, coupling):
    top_bit = lax.axis_size(BITS).bit_length() - 2
    parity = (lax.axis_index(BITS) >> top_bit & 1).astype(jnp.int32).reshape(1)
    keep, send = group_a(parity, boundary[0], gate_stack, coupling, CYC_A)
    recv = partner(send, BITS, top_bit)
    cols = group_b(parity, keep, recv, gate_stack, coupling, CYC_B)
    cols = swap_lanes(reduce_columns(cols), 0)
    width = cols.shape[0]
    col_start = lax.axis_index(CUTS) * width
    cpl_base = CYC_A + CYC_B
    tables = lax.dynamic_slice_in_dim(coupling[cpl_base:cpl_base + CYC_C], col_start, width, axis=2)
    return final_layers(cols, gate_stack, jnp.swapaxes(tables, 1, 2), 3 * CYC_A + 3 * CYC_B, CYC_C)


def solution(mesh):
    n_bits, n_cuts = mesh.shape["bits"], mesh.shape["cuts"]
    fine = Mesh(mesh.devices.reshape(2, n_bits // 4, 2, n_cuts // 4, 4), BITS + CUTS)
    in_specs = (P(CUTS, BITS, None), P(), P())
    out_specs = P(BITS, CUTS)
    return jax.shard_map(
        on_device, mesh=fine, in_specs=in_specs, out_specs=out_specs, check_vma=False
    )
```

```python
import functools

import jax
import jax.numpy as jnp
from jax import lax
from jax.experimental import pallas as pl
from jax.experimental.pallas import tpu as pltpu
from jax.sharding import Mesh, PartitionSpec as P

CYC_A = 4
CYC_B = 4
CYC_C = 5
BITS = ("yh", "z", "core")
CUTS = ("x", "yl")

BLOCK = 128


def _split(a):
    hi = a.astype(jnp.bfloat16)
    lo = (a - hi.astype(jnp.float32)).astype(jnp.bfloat16)
    return hi, lo


def _weights(g):
    hi, lo = _split(0.45 * g)
    return jnp.concatenate([hi, hi, lo], axis=0)


def _apply(x, w):
    hi, lo = _split(x)
    lhs = jnp.concatenate([hi, lo, hi], axis=1)
    return 0.9 * x + jnp.dot(lhs, w, preferred_element_type=jnp.float32)


def _weights_left(g):
    hi, lo = _split((0.45 * g).T)
    return jnp.concatenate([hi, lo, hi], axis=1)


def _apply_left(w, x):
    hi, lo = _split(x)
    rhs = jnp.concatenate([hi, hi, lo], axis=0)
    return 0.9 * x + jnp.dot(w, rhs, preferred_element_type=jnp.float32)


def _layer_turns(o_ref, t_ref, g_ref, c_ref, cycles, last_to=None):
    rows = o_ref.shape[0]
    n_blocks = rows // BLOCK
    for turn in range(cycles):
        first = 3 * turn
        table = c_ref[turn]
        xs = jnp.concatenate([o_ref[pl.ds(t, BLOCK, stride=n_blocks), :] for t in range(n_blocks)], axis=1)
        ys = _apply_left(_weights_left(g_ref[first]), xs)
        for t in range(n_blocks):
            o_ref[pl.ds(t, BLOCK, stride=n_blocks), :] = ys[:, t * BLOCK:(t + 1) * BLOCK]
        y = _apply(o_ref[...], _weights(g_ref[first + 1]))
        o_ref[...] = (y.reshape(n_blocks, BLOCK, -1) * table[None]).reshape(y.shape)
        if last_to is not None and turn == cycles - 1:
            for a in range(n_blocks):
                t_ref[pl.ds(a * BLOCK, BLOCK), :] = o_ref[pl.ds(a * BLOCK, BLOCK), :].T
            t_ref[...] = _apply(t_ref[...], _weights(g_ref[first + 2]))
            for a in range(n_blocks):
                last_to[:, pl.ds(a * BLOCK, BLOCK)] = t_ref[pl.ds(a * BLOCK, BLOCK), :]
        else:
            xs = jnp.concatenate([o_ref[pl.ds(a * BLOCK, BLOCK), :] for a in range(n_blocks)], axis=1)
            ys = _apply_left(_weights_left(g_ref[first + 2]), xs)
            for a in range(n_blocks):
                o_ref[pl.ds(a * BLOCK, BLOCK), :] = ys[:, a * BLOCK:(a + 1) * BLOCK]


def _group_a_kernel(p_ref, x_ref, g_ref, c_ref, keep_ref, send_ref, o_ref, *, cycles):
    half = keep_ref.shape[0]
    o_ref[...] = x_ref[...]
    _layer_turns(o_ref, None, g_ref, c_ref, cycles)
    p = p_ref[0]
    keep_ref[...] = o_ref[pl.ds(pl.multiple_of(p * half, half), half), :]
    send_ref[...] = o_ref[pl.ds(pl.multiple_of((1 - p) * half, half), half), :]


def _group_b_kernel(p_ref, keep_ref, recv_ref, g_ref, c_ref, out_ref, o_ref, t_ref, *, cycles):
    half = keep_ref.shape[0]
    p = p_ref[0]
    o_ref[pl.ds(pl.multiple_of(p * half, half), half), :] = keep_ref[...]
    o_ref[pl.ds(pl.multiple_of((1 - p) * half, half), half), :] = recv_ref[...]
    _layer_turns(o_ref, t_ref, g_ref, c_ref, cycles, last_to=out_ref)


def _smem():
    return pl.BlockSpec(memory_space=pltpu.SMEM)


def _vmem():
    return pl.BlockSpec(memory_space=pltpu.VMEM)


def _stack_block(count, index):
    return pl.BlockSpec((count, BLOCK, BLOCK), lambda step: (index, 0, 0), memory_space=pltpu.VMEM)


def group_a(parity, x, gate_stack, coupling, cycles):
    half = jax.ShapeDtypeStruct((x.shape[0] // 2, x.shape[1]), x.dtype)
    return pl.pallas_call(
        functools.partial(_group_a_kernel, cycles=cycles),
        out_shape=(half, half),
        grid=(1,),
        in_specs=[_smem(), _vmem(), _stack_block(3 * cycles, 0), _stack_block(cycles, 0)],
        out_specs=(_vmem(), _vmem()),
        scratch_shapes=[pltpu.VMEM(x.shape, jnp.float32)],
    )(parity, x, gate_stack, coupling)


def group_b(parity, keep, recv, gate_stack, coupling, cycles):
    rows, cols = keep.shape[0] * 2, keep.shape[1]
    return pl.pallas_call(
        functools.partial(_group_b_kernel, cycles=cycles),
        out_shape=jax.ShapeDtypeStruct((cols, rows), keep.dtype),
        grid=(1,),
        in_specs=[_smem(), _vmem(), _vmem(), _stack_block(3 * cycles, 1), _stack_block(cycles, 1)],
        out_specs=_vmem(),
        scratch_shapes=[pltpu.VMEM((rows, cols), jnp.float32), pltpu.VMEM((rows, cols), jnp.float32)],
    )(parity, keep, recv, gate_stack, coupling)


def _final_kernel(p_ref, d_ref, recv_ref, g_ref, tab_ref, out_ref, o_ref, m_ref, *, cycles):
    width = d_ref.shape[0]
    n_blocks = d_ref.shape[1] // BLOCK
    half = n_blocks // 2
    p = p_ref[0]
    for a in range(n_blocks):
        lane_block = pl.ds(a * BLOCK, BLOCK)
        other = pl.ds((a % half) * BLOCK, BLOCK)
        own = d_ref[:, lane_block]
        got = recv_ref[:, other]
        keep = (a // half) == p
        o_ref[lane_block, :] = jnp.where(keep, own, got).T
    for turn in range(cycles):
        for t in range(n_blocks):
            m_ref[pl.ds(t * width, width), :] = o_ref[pl.ds(t, BLOCK, stride=n_blocks), :].T
        m_ref[...] = _apply(m_ref[...], _weights(g_ref[2 * turn]))
        for t in range(n_blocks):
            o_ref[pl.ds(t, BLOCK, stride=n_blocks), :] = m_ref[pl.ds(t * width, width), :].T
        table = tab_ref[turn]
        for a in range(n_blocks):
            m_ref[pl.ds(a * width, width), :] = o_ref[pl.ds(a * BLOCK, BLOCK), :].T * table
        m_ref[...] = _apply(m_ref[...], _weights(g_ref[2 * turn + 1]))
        for a in range(n_blocks):
            if turn == cycles - 1:
                out_ref[:, pl.ds(a * BLOCK, BLOCK)] = m_ref[pl.ds(a * width, width), :]
            else:
                o_ref[pl.ds(a * BLOCK, BLOCK), :] = m_ref[pl.ds(a * width, width), :].T


def final_layers(parity, cols, recv, gates, tables, cycles):
    width, rows = cols.shape
    out = pl.pallas_call(
        functools.partial(_final_kernel, cycles=cycles),
        out_shape=jax.ShapeDtypeStruct((width, rows), cols.dtype),
        in_specs=[_smem(), _vmem(), _vmem(), _vmem(), _vmem()],
        out_specs=_vmem(),
        scratch_shapes=[pltpu.VMEM((rows, width), jnp.float32), pltpu.VMEM((BLOCK, BLOCK), jnp.float32)],
    )(parity, cols, recv, gates, tables)
    return out.T


HIGHEST_PREC = lax.Precision.HIGHEST


def partner(value, axis, distance):
    mask = 2**distance
    pairs = [(source, source ^ mask) for source in range(lax.axis_size(axis))]
    return lax.ppermute(value, axis, pairs)


def effective(weight_mat):
    order_size = weight_mat.shape[0]
    return 0.9 * jnp.eye(order_size, dtype=weight_mat.dtype) + 0.45 * weight_mat


def apply_lane(tensor, weight_mat):
    return jnp.dot(tensor, effective(weight_mat), precision=HIGHEST_PREC)


def apply_mid(tensor, weight_mat):
    order_size = weight_mat.shape[0]
    shaped = tensor.reshape(-1, order_size, tensor.shape[1])
    mixed = jnp.einsum("aic,ij->ajc", shaped, effective(weight_mat), precision=HIGHEST_PREC)
    return mixed.reshape(tensor.shape)


def apply_top(tensor, weight_mat):
    order_size = weight_mat.shape[0]
    shaped = tensor.reshape(order_size, -1)
    mixed = jnp.dot(effective(weight_mat).T, shaped, precision=HIGHEST_PREC)
    return mixed.reshape(tensor.shape)


def apply_couple(tensor, table):
    shaped = tensor.reshape(-1, table.shape[0], tensor.shape[1])
    return (shaped * table[None]).reshape(tensor.shape)


def layer_group(tensor, gate_stack, coupling, gate_base, cpl_base, cycles):
    for turn_index in range(cycles):
        first = gate_base + 3 * turn_index
        tensor = apply_top(tensor, gate_stack[first])
        tensor = apply_lane(tensor, gate_stack[first + 1])
        tensor = apply_couple(tensor, coupling[cpl_base + turn_index])
        tensor = apply_mid(tensor, gate_stack[first + 2])
    return tensor


def final_group_cols(cols, gate_stack, coupling, col_start):
    order_size = gate_stack.shape[1]
    width = cols.shape[0]
    gate_base = 3 * CYC_A + 3 * CYC_B
    cpl_base = CYC_A + CYC_B
    for turn_index in range(CYC_C):
        top_mat = effective(gate_stack[gate_base + 2 * turn_index])
        shaped = cols.reshape(width, order_size, -1)
        cols = jnp.einsum("cit,ij->cjt", shaped, top_mat, precision=HIGHEST_PREC).reshape(cols.shape)
        table = lax.dynamic_slice_in_dim(coupling[cpl_base + turn_index], col_start, width, axis=1)
        shaped = cols.reshape(width, -1, order_size)
        cols = (shaped * table.T[:, None, :]).reshape(cols.shape)
        mid_mat = effective(gate_stack[gate_base + 2 * turn_index + 1])
        cols = jnp.dot(cols.reshape(-1, order_size), mid_mat, precision=HIGHEST_PREC).reshape(cols.shape)
    return cols


def swap_bit(tensor, bit_pos):
    half_rows = tensor.shape[0] // 2
    lower = tensor[:half_rows]
    upper = tensor[half_rows:]
    parity = lax.axis_index(BITS) >> bit_pos & 1
    outgoing = jnp.where(parity == 0, upper, lower)
    incoming = partner(outgoing, BITS, bit_pos)
    return jnp.where(
        parity == 0, jnp.concatenate([lower, incoming], 0), jnp.concatenate([incoming, upper], 0)
    )


def reduce_columns(cols):
    for axis in ("x", "yl"):
        n = lax.axis_size(axis)
        blocks = cols.reshape(n, cols.shape[0] // n, cols.shape[1])
        cols = lax.all_to_all(blocks, axis, 0, 0, tiled=False).sum(0)
    return cols


def swap_lanes(cols, bit_pos):
    half = cols.shape[1] // 2
    lower = cols[:, :half]
    upper = cols[:, half:]
    parity = lax.axis_index(BITS) >> bit_pos & 1
    outgoing = jnp.where(parity == 0, upper, lower)
    incoming = partner(outgoing, BITS, bit_pos)
    return jnp.where(
        parity == 0, jnp.concatenate([lower, incoming], 1), jnp.concatenate([incoming, upper], 1)
    )


def on_device(boundary, gate_stack, coupling):
    top_bit = lax.axis_size(BITS).bit_length() - 2
    parity = (lax.axis_index(BITS) >> top_bit & 1).astype(jnp.int32).reshape(1)
    keep, send = group_a(parity, boundary[0], gate_stack, coupling, CYC_A)
    recv = partner(send, BITS, top_bit)
    cols = reduce_columns(group_b(parity, keep, recv, gate_stack, coupling, CYC_B))
    half = cols.shape[1] // 2
    low = (lax.axis_index(BITS) & 1).astype(jnp.int32).reshape(1)
    outgoing = jnp.where(low[0] == 0, cols[:, half:], cols[:, :half])
    incoming = partner(outgoing, BITS, 0)
    width = cols.shape[0]
    col_start = lax.axis_index(CUTS) * width
    gate_base, cpl_base = 3 * CYC_A + 3 * CYC_B, CYC_A + CYC_B
    tables = lax.dynamic_slice_in_dim(coupling[cpl_base:cpl_base + CYC_C], col_start, width, axis=2)
    gates = gate_stack[gate_base:gate_base + 2 * CYC_C]
    return final_layers(low, cols, incoming, gates, jnp.swapaxes(tables, 1, 2), CYC_C)


def solution(mesh):
    n_bits, n_cuts = mesh.shape["bits"], mesh.shape["cuts"]
    fine = Mesh(mesh.devices.reshape(2, n_bits // 4, 2, n_cuts // 4, 4), BITS + CUTS)
    in_specs = (P(CUTS, BITS, None), P(), P())
    out_specs = P(BITS, CUTS)
    return jax.shard_map(
        on_device, mesh=fine, in_specs=in_specs, out_specs=out_specs, check_vma=False
    )
```

```python
import functools

import jax
import jax.numpy as jnp
from jax import lax
from jax.experimental import pallas as pl
from jax.experimental.pallas import tpu as pltpu
from jax.sharding import Mesh, PartitionSpec as P

CYC_A = 4
CYC_B = 4
CYC_C = 5
BITS = ("yh", "z", "core")
CUTS = ("x", "yl")

BLOCK = 128


def _split(a):
    hi = a.astype(jnp.bfloat16)
    lo = (a - hi.astype(jnp.float32)).astype(jnp.bfloat16)
    return hi, lo


def _weights(g):
    hi, lo = _split(0.45 * g)
    return jnp.concatenate([hi, hi, lo], axis=0)


def _apply(x, w):
    hi, lo = _split(x)
    lhs = jnp.concatenate([hi, lo, hi], axis=1)
    return 0.9 * x + jnp.dot(lhs, w, preferred_element_type=jnp.float32)


def _weights_left(g):
    hi, lo = _split((0.45 * g).T)
    return jnp.concatenate([hi, lo, hi], axis=1)


def _apply_left(w, x):
    hi, lo = _split(x)
    rhs = jnp.concatenate([hi, hi, lo], axis=0)
    return 0.9 * x + jnp.dot(w, rhs, preferred_element_type=jnp.float32)


def _layer_turns(o_ref, t_ref, g_ref, c_ref, cycles, last_to=None):
    rows = o_ref.shape[0]
    n_blocks = rows // BLOCK
    for turn in range(cycles):
        first = 3 * turn
        table = c_ref[turn]
        xs = jnp.concatenate([o_ref[pl.ds(t, BLOCK, stride=n_blocks), :] for t in range(n_blocks)], axis=1)
        ys = _apply_left(_weights_left(g_ref[first]), xs)
        for t in range(n_blocks):
            o_ref[pl.ds(t, BLOCK, stride=n_blocks), :] = ys[:, t * BLOCK:(t + 1) * BLOCK]
        y = _apply(o_ref[...], _weights(g_ref[first + 1]))
        o_ref[...] = (y.reshape(n_blocks, BLOCK, -1) * table[None]).reshape(y.shape)
        if last_to is not None and turn == cycles - 1:
            for a in range(n_blocks):
                t_ref[pl.ds(a * BLOCK, BLOCK), :] = o_ref[pl.ds(a * BLOCK, BLOCK), :].T
            t_ref[...] = _apply(t_ref[...], _weights(g_ref[first + 2]))
            for a in range(n_blocks):
                last_to[:, pl.ds(a * BLOCK, BLOCK)] = t_ref[pl.ds(a * BLOCK, BLOCK), :]
        else:
            xs = jnp.concatenate([o_ref[pl.ds(a * BLOCK, BLOCK), :] for a in range(n_blocks)], axis=1)
            ys = _apply_left(_weights_left(g_ref[first + 2]), xs)
            for a in range(n_blocks):
                o_ref[pl.ds(a * BLOCK, BLOCK), :] = ys[:, a * BLOCK:(a + 1) * BLOCK]


def _group_a_kernel(p_ref, x_ref, g_ref, c_ref, keep_ref, send_ref, o_ref, *, cycles):
    half = keep_ref.shape[0]
    o_ref[...] = x_ref[...]
    _layer_turns(o_ref, None, g_ref, c_ref, cycles)
    p = p_ref[0]
    keep_ref[...] = o_ref[pl.ds(pl.multiple_of(p * half, half), half), :]
    send_ref[...] = o_ref[pl.ds(pl.multiple_of((1 - p) * half, half), half), :]


def _group_b_kernel(p_ref, keep_ref, recv_ref, g_ref, c_ref, out_ref, o_ref, t_ref, *, cycles):
    half = keep_ref.shape[0]
    p = p_ref[0]
    o_ref[pl.ds(pl.multiple_of(p * half, half), half), :] = keep_ref[...]
    o_ref[pl.ds(pl.multiple_of((1 - p) * half, half), half), :] = recv_ref[...]
    _layer_turns(o_ref, t_ref, g_ref, c_ref, cycles, last_to=out_ref)


def _smem():
    return pl.BlockSpec(memory_space=pltpu.SMEM)


def _vmem():
    return pl.BlockSpec(memory_space=pltpu.VMEM)


def _stack_block(count, index):
    return pl.BlockSpec((count, BLOCK, BLOCK), lambda step: (index, 0, 0), memory_space=pltpu.VMEM)


def group_a(parity, x, gate_stack, coupling, cycles):
    half = jax.ShapeDtypeStruct((x.shape[0] // 2, x.shape[1]), x.dtype)
    return pl.pallas_call(
        functools.partial(_group_a_kernel, cycles=cycles),
        out_shape=(half, half),
        grid=(1,),
        in_specs=[_smem(), _vmem(), _stack_block(3 * cycles, 0), _stack_block(cycles, 0)],
        out_specs=(_vmem(), _vmem()),
        scratch_shapes=[pltpu.VMEM(x.shape, jnp.float32)],
    )(parity, x, gate_stack, coupling)


def group_b(parity, keep, recv, gate_stack, coupling, cycles):
    rows, cols = keep.shape[0] * 2, keep.shape[1]
    return pl.pallas_call(
        functools.partial(_group_b_kernel, cycles=cycles),
        out_shape=jax.ShapeDtypeStruct((cols, rows), keep.dtype),
        grid=(1,),
        in_specs=[_smem(), _vmem(), _vmem(), _stack_block(3 * cycles, 1), _stack_block(cycles, 1)],
        out_specs=_vmem(),
        scratch_shapes=[pltpu.VMEM((rows, cols), jnp.float32), pltpu.VMEM((rows, cols), jnp.float32)],
    )(parity, keep, recv, gate_stack, coupling)


def _final_kernel(p_ref, d_ref, recv_ref, g_ref, tab_ref, out_ref, o_ref, m_ref, *, gate_base, cycles):
    width = d_ref.shape[0]
    n_blocks = d_ref.shape[1] // BLOCK
    half = n_blocks // 2
    p = p_ref[0]
    for a in range(n_blocks):
        lane_block = pl.ds(a * BLOCK, BLOCK)
        other = pl.ds((a % half) * BLOCK, BLOCK)
        own = d_ref[:, lane_block]
        got = recv_ref[:, other]
        keep = (a // half) == p
        o_ref[lane_block, :] = jnp.where(keep, own, got).T
    for turn in range(cycles):
        for t in range(n_blocks):
            m_ref[pl.ds(t * width, width), :] = o_ref[pl.ds(t, BLOCK, stride=n_blocks), :].T
        m_ref[...] = _apply(m_ref[...], _weights(g_ref[gate_base + 2 * turn]))
        for t in range(n_blocks):
            o_ref[pl.ds(t, BLOCK, stride=n_blocks), :] = m_ref[pl.ds(t * width, width), :].T
        table = tab_ref[turn]
        for a in range(n_blocks):
            m_ref[pl.ds(a * width, width), :] = o_ref[pl.ds(a * BLOCK, BLOCK), :].T * table
        m_ref[...] = _apply(m_ref[...], _weights(g_ref[gate_base + 2 * turn + 1]))
        for a in range(n_blocks):
            if turn == cycles - 1:
                out_ref[:, pl.ds(a * BLOCK, BLOCK)] = m_ref[pl.ds(a * width, width), :]
            else:
                o_ref[pl.ds(a * BLOCK, BLOCK), :] = m_ref[pl.ds(a * width, width), :].T


def final_layers(parity, cols, recv, gate_stack, tables, gate_base, cycles):
    width, rows = cols.shape
    out = pl.pallas_call(
        functools.partial(_final_kernel, gate_base=gate_base, cycles=cycles),
        out_shape=jax.ShapeDtypeStruct((width, rows), cols.dtype),
        in_specs=[_smem(), _vmem(), _vmem(), _vmem(), _vmem()],
        out_specs=_vmem(),
        scratch_shapes=[pltpu.VMEM((rows, width), jnp.float32), pltpu.VMEM((BLOCK, BLOCK), jnp.float32)],
    )(parity, cols, recv, gate_stack, tables)
    return out.T


HIGHEST_PREC = lax.Precision.HIGHEST


def partner(value, axis, distance):
    mask = 2**distance
    pairs = [(source, source ^ mask) for source in range(lax.axis_size(axis))]
    return lax.ppermute(value, axis, pairs)


def effective(weight_mat):
    order_size = weight_mat.shape[0]
    return 0.9 * jnp.eye(order_size, dtype=weight_mat.dtype) + 0.45 * weight_mat


def apply_lane(tensor, weight_mat):
    return jnp.dot(tensor, effective(weight_mat), precision=HIGHEST_PREC)


def apply_mid(tensor, weight_mat):
    order_size = weight_mat.shape[0]
    shaped = tensor.reshape(-1, order_size, tensor.shape[1])
    mixed = jnp.einsum("aic,ij->ajc", shaped, effective(weight_mat), precision=HIGHEST_PREC)
    return mixed.reshape(tensor.shape)


def apply_top(tensor, weight_mat):
    order_size = weight_mat.shape[0]
    shaped = tensor.reshape(order_size, -1)
    mixed = jnp.dot(effective(weight_mat).T, shaped, precision=HIGHEST_PREC)
    return mixed.reshape(tensor.shape)


def apply_couple(tensor, table):
    shaped = tensor.reshape(-1, table.shape[0], tensor.shape[1])
    return (shaped * table[None]).reshape(tensor.shape)


def layer_group(tensor, gate_stack, coupling, gate_base, cpl_base, cycles):
    for turn_index in range(cycles):
        first = gate_base + 3 * turn_index
        tensor = apply_top(tensor, gate_stack[first])
        tensor = apply_lane(tensor, gate_stack[first + 1])
        tensor = apply_couple(tensor, coupling[cpl_base + turn_index])
        tensor = apply_mid(tensor, gate_stack[first + 2])
    return tensor


def final_group_cols(cols, gate_stack, coupling, col_start):
    order_size = gate_stack.shape[1]
    width = cols.shape[0]
    gate_base = 3 * CYC_A + 3 * CYC_B
    cpl_base = CYC_A + CYC_B
    for turn_index in range(CYC_C):
        top_mat = effective(gate_stack[gate_base + 2 * turn_index])
        shaped = cols.reshape(width, order_size, -1)
        cols = jnp.einsum("cit,ij->cjt", shaped, top_mat, precision=HIGHEST_PREC).reshape(cols.shape)
        table = lax.dynamic_slice_in_dim(coupling[cpl_base + turn_index], col_start, width, axis=1)
        shaped = cols.reshape(width, -1, order_size)
        cols = (shaped * table.T[:, None, :]).reshape(cols.shape)
        mid_mat = effective(gate_stack[gate_base + 2 * turn_index + 1])
        cols = jnp.dot(cols.reshape(-1, order_size), mid_mat, precision=HIGHEST_PREC).reshape(cols.shape)
    return cols


def swap_bit(tensor, bit_pos):
    half_rows = tensor.shape[0] // 2
    lower = tensor[:half_rows]
    upper = tensor[half_rows:]
    parity = lax.axis_index(BITS) >> bit_pos & 1
    outgoing = jnp.where(parity == 0, upper, lower)
    incoming = partner(outgoing, BITS, bit_pos)
    return jnp.where(
        parity == 0, jnp.concatenate([lower, incoming], 0), jnp.concatenate([incoming, upper], 0)
    )


def reduce_columns(cols):
    for axis in ("x", "yl"):
        n = lax.axis_size(axis)
        blocks = cols.reshape(n, cols.shape[0] // n, cols.shape[1])
        cols = lax.all_to_all(blocks, axis, 0, 0, tiled=False).sum(0)
    return cols


def swap_lanes(cols, bit_pos):
    half = cols.shape[1] // 2
    lower = cols[:, :half]
    upper = cols[:, half:]
    parity = lax.axis_index(BITS) >> bit_pos & 1
    outgoing = jnp.where(parity == 0, upper, lower)
    incoming = partner(outgoing, BITS, bit_pos)
    return jnp.where(
        parity == 0, jnp.concatenate([lower, incoming], 1), jnp.concatenate([incoming, upper], 1)
    )


def on_device(boundary, gate_stack, coupling):
    top_bit = lax.axis_size(BITS).bit_length() - 2
    parity = (lax.axis_index(BITS) >> top_bit & 1).astype(jnp.int32).reshape(1)
    keep, send = group_a(parity, boundary[0], gate_stack, coupling, CYC_A)
    recv = partner(send, BITS, top_bit)
    cols = reduce_columns(group_b(parity, keep, recv, gate_stack, coupling, CYC_B))
    half = cols.shape[1] // 2
    low = (lax.axis_index(BITS) & 1).astype(jnp.int32).reshape(1)
    outgoing = jnp.where(low[0] == 0, cols[:, half:], cols[:, :half])
    incoming = partner(outgoing, BITS, 0)
    width = cols.shape[0]
    col_start = lax.axis_index(CUTS) * width
    gate_base, cpl_base = 3 * CYC_A + 3 * CYC_B, CYC_A + CYC_B
    tables = lax.dynamic_slice_in_dim(coupling[cpl_base:cpl_base + CYC_C], col_start, width, axis=2)
    return final_layers(low, cols, incoming, gate_stack, jnp.swapaxes(tables, 1, 2), gate_base, CYC_C)


def solution(mesh):
    n_bits, n_cuts = mesh.shape["bits"], mesh.shape["cuts"]
    fine = Mesh(mesh.devices.reshape(2, n_bits // 4, 2, n_cuts // 4, 4), BITS + CUTS)
    in_specs = (P(CUTS, BITS, None), P(), P())
    out_specs = P(BITS, CUTS)
    return jax.shard_map(
        on_device, mesh=fine, in_specs=in_specs, out_specs=out_specs, check_vma=False
    )
```

```python
import functools

import jax
import jax.numpy as jnp
from jax import lax
from jax.experimental import pallas as pl
from jax.experimental.pallas import tpu as pltpu
from jax.sharding import Mesh, PartitionSpec as P

CYC_A = 4
CYC_B = 4
CYC_C = 5
BITS = ("yh", "z", "core")
CUTS = ("x", "yl")

BLOCK = 128


def _split(a):
    hi = a.astype(jnp.bfloat16)
    lo = (a - hi.astype(jnp.float32)).astype(jnp.bfloat16)
    return hi, lo


def _weights(g):
    hi, lo = _split(0.45 * g)
    return jnp.concatenate([hi, hi, lo], axis=0)


def _apply(x, w):
    hi, lo = _split(x)
    lhs = jnp.concatenate([hi, lo, hi], axis=1)
    return 0.9 * x + jnp.dot(lhs, w, preferred_element_type=jnp.float32)


def _weights_left(g):
    hi, lo = _split((0.45 * g).T)
    return jnp.concatenate([hi, lo, hi], axis=1)


def _apply_left(w, x):
    hi, lo = _split(x)
    rhs = jnp.concatenate([hi, hi, lo], axis=0)
    return 0.9 * x + jnp.dot(w, rhs, preferred_element_type=jnp.float32)


def _layer_turns(o_ref, t_ref, g_ref, c_ref, cycles, last_to=None):
    rows = o_ref.shape[0]
    n_blocks = rows // BLOCK
    for turn in range(cycles):
        first = 3 * turn
        table = c_ref[turn]
        xs = jnp.concatenate([o_ref[pl.ds(t, BLOCK, stride=n_blocks), :] for t in range(n_blocks)], axis=1)
        ys = _apply_left(_weights_left(g_ref[first]), xs)
        for t in range(n_blocks):
            o_ref[pl.ds(t, BLOCK, stride=n_blocks), :] = ys[:, t * BLOCK:(t + 1) * BLOCK]
        y = _apply(o_ref[...], _weights(g_ref[first + 1]))
        o_ref[...] = (y.reshape(n_blocks, BLOCK, -1) * table[None]).reshape(y.shape)
        if last_to is not None and turn == cycles - 1:
            for a in range(n_blocks):
                t_ref[pl.ds(a * BLOCK, BLOCK), :] = o_ref[pl.ds(a * BLOCK, BLOCK), :].T
            t_ref[...] = _apply(t_ref[...], _weights(g_ref[first + 2]))
            for a in range(n_blocks):
                last_to[:, pl.ds(a * BLOCK, BLOCK)] = t_ref[pl.ds(a * BLOCK, BLOCK), :]
        else:
            xs = jnp.concatenate([o_ref[pl.ds(a * BLOCK, BLOCK), :] for a in range(n_blocks)], axis=1)
            ys = _apply_left(_weights_left(g_ref[first + 2]), xs)
            for a in range(n_blocks):
                o_ref[pl.ds(a * BLOCK, BLOCK), :] = ys[:, a * BLOCK:(a + 1) * BLOCK]


def _group_a_kernel(p_ref, x_ref, g_ref, c_ref, keep_ref, send_ref, o_ref, *, cycles):
    half = keep_ref.shape[0]
    o_ref[...] = x_ref[...]
    _layer_turns(o_ref, None, g_ref, c_ref, cycles)
    p = p_ref[0]
    keep_ref[...] = o_ref[pl.ds(pl.multiple_of(p * half, half), half), :]
    send_ref[...] = o_ref[pl.ds(pl.multiple_of((1 - p) * half, half), half), :]


def _group_b_kernel(p_ref, keep_ref, recv_ref, g_ref, c_ref, out_ref, o_ref, t_ref, *, cycles):
    half = keep_ref.shape[0]
    p = p_ref[0]
    o_ref[pl.ds(pl.multiple_of(p * half, half), half), :] = keep_ref[...]
    o_ref[pl.ds(pl.multiple_of((1 - p) * half, half), half), :] = recv_ref[...]
    _layer_turns(o_ref, t_ref, g_ref, c_ref, cycles, last_to=out_ref)


def _smem():
    return pl.BlockSpec(memory_space=pltpu.SMEM)


def _vmem():
    return pl.BlockSpec(memory_space=pltpu.VMEM)


def _stack_block(count, index):
    return pl.BlockSpec((count, BLOCK, BLOCK), lambda step: (index, 0, 0), memory_space=pltpu.VMEM)


def group_a(parity, x, gate_stack, coupling, cycles):
    half = jax.ShapeDtypeStruct((x.shape[0] // 2, x.shape[1]), x.dtype)
    return pl.pallas_call(
        functools.partial(_group_a_kernel, cycles=cycles),
        out_shape=(half, half),
        grid=(1,),
        in_specs=[_smem(), _vmem(), _stack_block(3 * cycles, 0), _stack_block(cycles, 0)],
        out_specs=(_vmem(), _vmem()),
        scratch_shapes=[pltpu.VMEM(x.shape, jnp.float32)],
    )(parity, x, gate_stack, coupling)


def group_b(parity, keep, recv, gate_stack, coupling, cycles):
    rows, cols = keep.shape[0] * 2, keep.shape[1]
    return pl.pallas_call(
        functools.partial(_group_b_kernel, cycles=cycles),
        out_shape=jax.ShapeDtypeStruct((cols, rows), keep.dtype),
        grid=(1,),
        in_specs=[_smem(), _vmem(), _vmem(), _stack_block(3 * cycles, 1), _stack_block(cycles, 1)],
        out_specs=_vmem(),
        scratch_shapes=[pltpu.VMEM((rows, cols), jnp.float32), pltpu.VMEM((rows, cols), jnp.float32)],
    )(parity, keep, recv, gate_stack, coupling)


def _final_kernel(p_ref, d_ref, recv_ref, g_ref, c_ref, out_ref, o_ref, m_ref, tt_ref, *, gate_base, cpl_base, cycles):
    width = d_ref.shape[0]
    n_blocks = d_ref.shape[1] // BLOCK
    half = n_blocks // 2
    p = p_ref[0]
    col_start = pl.multiple_of(p_ref[1] * width, width)
    for a in range(n_blocks):
        lane_block = pl.ds(a * BLOCK, BLOCK)
        other = pl.ds((a % half) * BLOCK, BLOCK)
        own = d_ref[:, lane_block]
        got = recv_ref[:, other]
        keep = (a // half) == p
        o_ref[lane_block, :] = jnp.where(keep, own, got).T
    for turn in range(cycles):
        for t in range(n_blocks):
            m_ref[pl.ds(t * width, width), :] = o_ref[pl.ds(t, BLOCK, stride=n_blocks), :].T
        m_ref[...] = _apply(m_ref[...], _weights(g_ref[gate_base + 2 * turn]))
        for t in range(n_blocks):
            o_ref[pl.ds(t, BLOCK, stride=n_blocks), :] = m_ref[pl.ds(t * width, width), :].T
        tt_ref[...] = c_ref[cpl_base + turn].T
        table = tt_ref[pl.ds(col_start, width), :]
        for a in range(n_blocks):
            m_ref[pl.ds(a * width, width), :] = o_ref[pl.ds(a * BLOCK, BLOCK), :].T * table
        m_ref[...] = _apply(m_ref[...], _weights(g_ref[gate_base + 2 * turn + 1]))
        for a in range(n_blocks):
            if turn == cycles - 1:
                out_ref[:, pl.ds(a * BLOCK, BLOCK)] = m_ref[pl.ds(a * width, width), :]
            else:
                o_ref[pl.ds(a * BLOCK, BLOCK), :] = m_ref[pl.ds(a * width, width), :].T


def final_layers(scalars, cols, recv, gate_stack, coupling, gate_base, cpl_base, cycles):
    width, rows = cols.shape
    kernel = functools.partial(_final_kernel, gate_base=gate_base, cpl_base=cpl_base, cycles=cycles)
    out = pl.pallas_call(
        kernel,
        out_shape=jax.ShapeDtypeStruct((width, rows), cols.dtype),
        in_specs=[_smem(), _vmem(), _vmem(), _vmem(), _vmem()],
        out_specs=_vmem(),
        scratch_shapes=[
            pltpu.VMEM((rows, width), jnp.float32),
            pltpu.VMEM((BLOCK, BLOCK), jnp.float32),
            pltpu.VMEM((BLOCK, BLOCK), jnp.float32),
        ],
    )(scalars, cols, recv, gate_stack, coupling)
    return out.T


HIGHEST_PREC = lax.Precision.HIGHEST


def partner(value, axis, distance):
    mask = 2**distance
    pairs = [(source, source ^ mask) for source in range(lax.axis_size(axis))]
    return lax.ppermute(value, axis, pairs)


def effective(weight_mat):
    order_size = weight_mat.shape[0]
    return 0.9 * jnp.eye(order_size, dtype=weight_mat.dtype) + 0.45 * weight_mat


def apply_lane(tensor, weight_mat):
    return jnp.dot(tensor, effective(weight_mat), precision=HIGHEST_PREC)


def apply_mid(tensor, weight_mat):
    order_size = weight_mat.shape[0]
    shaped = tensor.reshape(-1, order_size, tensor.shape[1])
    mixed = jnp.einsum("aic,ij->ajc", shaped, effective(weight_mat), precision=HIGHEST_PREC)
    return mixed.reshape(tensor.shape)


def apply_top(tensor, weight_mat):
    order_size = weight_mat.shape[0]
    shaped = tensor.reshape(order_size, -1)
    mixed = jnp.dot(effective(weight_mat).T, shaped, precision=HIGHEST_PREC)
    return mixed.reshape(tensor.shape)


def apply_couple(tensor, table):
    shaped = tensor.reshape(-1, table.shape[0], tensor.shape[1])
    return (shaped * table[None]).reshape(tensor.shape)


def layer_group(tensor, gate_stack, coupling, gate_base, cpl_base, cycles):
    for turn_index in range(cycles):
        first = gate_base + 3 * turn_index
        tensor = apply_top(tensor, gate_stack[first])
        tensor = apply_lane(tensor, gate_stack[first + 1])
        tensor = apply_couple(tensor, coupling[cpl_base + turn_index])
        tensor = apply_mid(tensor, gate_stack[first + 2])
    return tensor


def final_group_cols(cols, gate_stack, coupling, col_start):
    order_size = gate_stack.shape[1]
    width = cols.shape[0]
    gate_base = 3 * CYC_A + 3 * CYC_B
    cpl_base = CYC_A + CYC_B
    for turn_index in range(CYC_C):
        top_mat = effective(gate_stack[gate_base + 2 * turn_index])
        shaped = cols.reshape(width, order_size, -1)
        cols = jnp.einsum("cit,ij->cjt", shaped, top_mat, precision=HIGHEST_PREC).reshape(cols.shape)
        table = lax.dynamic_slice_in_dim(coupling[cpl_base + turn_index], col_start, width, axis=1)
        shaped = cols.reshape(width, -1, order_size)
        cols = (shaped * table.T[:, None, :]).reshape(cols.shape)
        mid_mat = effective(gate_stack[gate_base + 2 * turn_index + 1])
        cols = jnp.dot(cols.reshape(-1, order_size), mid_mat, precision=HIGHEST_PREC).reshape(cols.shape)
    return cols


def swap_bit(tensor, bit_pos):
    half_rows = tensor.shape[0] // 2
    lower = tensor[:half_rows]
    upper = tensor[half_rows:]
    parity = lax.axis_index(BITS) >> bit_pos & 1
    outgoing = jnp.where(parity == 0, upper, lower)
    incoming = partner(outgoing, BITS, bit_pos)
    return jnp.where(
        parity == 0, jnp.concatenate([lower, incoming], 0), jnp.concatenate([incoming, upper], 0)
    )


def reduce_columns(cols):
    for axis in ("x", "yl"):
        n = lax.axis_size(axis)
        blocks = cols.reshape(n, cols.shape[0] // n, cols.shape[1])
        cols = lax.all_to_all(blocks, axis, 0, 0, tiled=False).sum(0)
    return cols


def swap_lanes(cols, bit_pos):
    half = cols.shape[1] // 2
    lower = cols[:, :half]
    upper = cols[:, half:]
    parity = lax.axis_index(BITS) >> bit_pos & 1
    outgoing = jnp.where(parity == 0, upper, lower)
    incoming = partner(outgoing, BITS, bit_pos)
    return jnp.where(
        parity == 0, jnp.concatenate([lower, incoming], 1), jnp.concatenate([incoming, upper], 1)
    )


def on_device(boundary, gate_stack, coupling):
    top_bit = lax.axis_size(BITS).bit_length() - 2
    parity = (lax.axis_index(BITS) >> top_bit & 1).astype(jnp.int32).reshape(1)
    keep, send = group_a(parity, boundary[0], gate_stack, coupling, CYC_A)
    recv = partner(send, BITS, top_bit)
    cols = reduce_columns(group_b(parity, keep, recv, gate_stack, coupling, CYC_B))
    half = cols.shape[1] // 2
    low = (lax.axis_index(BITS) & 1).astype(jnp.int32).reshape(1)
    outgoing = jnp.where(low[0] == 0, cols[:, half:], cols[:, :half])
    incoming = partner(outgoing, BITS, 0)
    gate_base, cpl_base = 3 * CYC_A + 3 * CYC_B, CYC_A + CYC_B
    scalars = jnp.concatenate([low, lax.axis_index(CUTS).astype(jnp.int32).reshape(1)])
    return final_layers(scalars, cols, incoming, gate_stack, coupling, gate_base, cpl_base, CYC_C)


def solution(mesh):
    n_bits, n_cuts = mesh.shape["bits"], mesh.shape["cuts"]
    fine = Mesh(mesh.devices.reshape(2, n_bits // 4, 2, n_cuts // 4, 4), BITS + CUTS)
    in_specs = (P(CUTS, BITS, None), P(), P())
    out_specs = P(BITS, CUTS)
    return jax.shard_map(
        on_device, mesh=fine, in_specs=in_specs, out_specs=out_specs, check_vma=False
    )
```

```python
import functools

import jax
import jax.numpy as jnp
from jax import lax
from jax.experimental import pallas as pl
from jax.experimental.pallas import tpu as pltpu
from jax.sharding import Mesh, PartitionSpec as P

CYC_A = 4
CYC_B = 4
CYC_C = 5
BITS = ("yh", "z", "core")
CUTS = ("x", "yl")

BLOCK = 128


def _split(a):
    hi = a.astype(jnp.bfloat16)
    lo = (a - hi.astype(jnp.float32)).astype(jnp.bfloat16)
    return hi, lo


def _weights(g):
    hi, lo = _split(0.45 * g)
    return jnp.concatenate([hi, hi, lo], axis=0)


def _apply(x, w):
    hi, lo = _split(x)
    lhs = jnp.concatenate([hi, lo, hi], axis=1)
    return 0.9 * x + jnp.dot(lhs, w, preferred_element_type=jnp.float32)


def _weights_left(g):
    hi, lo = _split((0.45 * g).T)
    return jnp.concatenate([hi, lo, hi], axis=1)


def _apply_left(w, x):
    hi, lo = _split(x)
    rhs = jnp.concatenate([hi, hi, lo], axis=0)
    return 0.9 * x + jnp.dot(w, rhs, preferred_element_type=jnp.float32)


def _layer_turns(o_ref, t_ref, g_ref, c_ref, cycles, last_to=None):
    rows = o_ref.shape[0]
    n_blocks = rows // BLOCK
    for turn in range(cycles):
        first = 3 * turn
        table = c_ref[turn]
        xs = jnp.concatenate([o_ref[pl.ds(t, BLOCK, stride=n_blocks), :] for t in range(n_blocks)], axis=1)
        ys = _apply_left(_weights_left(g_ref[first]), xs)
        for t in range(n_blocks):
            o_ref[pl.ds(t, BLOCK, stride=n_blocks), :] = ys[:, t * BLOCK:(t + 1) * BLOCK]
        y = _apply(o_ref[...], _weights(g_ref[first + 1]))
        o_ref[...] = (y.reshape(n_blocks, BLOCK, -1) * table[None]).reshape(y.shape)
        if last_to is not None and turn == cycles - 1:
            for a in range(n_blocks):
                t_ref[pl.ds(a * BLOCK, BLOCK), :] = o_ref[pl.ds(a * BLOCK, BLOCK), :].T
            t_ref[...] = _apply(t_ref[...], _weights(g_ref[first + 2]))
            for a in range(n_blocks):
                last_to[:, pl.ds(a * BLOCK, BLOCK)] = t_ref[pl.ds(a * BLOCK, BLOCK), :]
        else:
            xs = jnp.concatenate([o_ref[pl.ds(a * BLOCK, BLOCK), :] for a in range(n_blocks)], axis=1)
            ys = _apply_left(_weights_left(g_ref[first + 2]), xs)
            for a in range(n_blocks):
                o_ref[pl.ds(a * BLOCK, BLOCK), :] = ys[:, a * BLOCK:(a + 1) * BLOCK]


def _group_a_kernel(p_ref, x_ref, g_ref, c_ref, keep_ref, send_ref, o_ref, *, cycles):
    half = keep_ref.shape[0]
    o_ref[...] = x_ref[...]
    _layer_turns(o_ref, None, g_ref, c_ref, cycles)
    p = p_ref[0]
    keep_ref[...] = o_ref[pl.ds(pl.multiple_of(p * half, half), half), :]
    send_ref[...] = o_ref[pl.ds(pl.multiple_of((1 - p) * half, half), half), :]


def _group_b_kernel(p_ref, keep_ref, recv_ref, g_ref, c_ref, out_ref, o_ref, t_ref, *, cycles):
    half = keep_ref.shape[0]
    p = p_ref[0]
    o_ref[pl.ds(pl.multiple_of(p * half, half), half), :] = keep_ref[...]
    o_ref[pl.ds(pl.multiple_of((1 - p) * half, half), half), :] = recv_ref[...]
    _layer_turns(o_ref, t_ref, g_ref, c_ref, cycles, last_to=out_ref)


def _smem():
    return pl.BlockSpec(memory_space=pltpu.SMEM)


def _vmem():
    return pl.BlockSpec(memory_space=pltpu.VMEM)


def _stack_block(count, index):
    return pl.BlockSpec((count, BLOCK, BLOCK), lambda step: (index, 0, 0), memory_space=pltpu.VMEM)


def group_a(parity, x, gate_stack, coupling, cycles):
    half = jax.ShapeDtypeStruct((x.shape[0] // 2, x.shape[1]), x.dtype)
    return pl.pallas_call(
        functools.partial(_group_a_kernel, cycles=cycles),
        out_shape=(half, half),
        grid=(1,),
        in_specs=[_smem(), _vmem(), _stack_block(3 * cycles, 0), _stack_block(cycles, 0)],
        out_specs=(_vmem(), _vmem()),
        scratch_shapes=[pltpu.VMEM(x.shape, jnp.float32)],
    )(parity, x, gate_stack, coupling)


def group_b(parity, keep, recv, gate_stack, coupling, cycles):
    rows, cols = keep.shape[0] * 2, keep.shape[1]
    return pl.pallas_call(
        functools.partial(_group_b_kernel, cycles=cycles),
        out_shape=jax.ShapeDtypeStruct((cols, rows), keep.dtype),
        grid=(1,),
        in_specs=[_smem(), _vmem(), _vmem(), _stack_block(3 * cycles, 1), _stack_block(cycles, 1)],
        out_specs=_vmem(),
        scratch_shapes=[pltpu.VMEM((rows, cols), jnp.float32), pltpu.VMEM((rows, cols), jnp.float32)],
    )(parity, keep, recv, gate_stack, coupling)


def _final_kernel(p_ref, cut_ref, d_ref, recv_hbm, g_ref, c_ref, out_ref, o_ref, m_ref, tt_ref, rv_ref, sem, *,
                  gate_base, cpl_base, cycles):
    width = d_ref.shape[0]
    n_blocks = d_ref.shape[1] // BLOCK
    half = n_blocks // 2
    half_rows = half * BLOCK
    p = p_ref[0]
    col_start = pl.multiple_of(cut_ref[0] * width, width)
    fetch = pltpu.make_async_copy(recv_hbm, rv_ref, sem)
    fetch.start()
    own_at = pl.multiple_of(p * half_rows, half_rows)
    got_at = pl.multiple_of((1 - p) * half_rows, half_rows)
    for a in range(half):
        lanes = pl.ds(pl.multiple_of(own_at + a * BLOCK, BLOCK), BLOCK)
        o_ref[pl.ds(pl.multiple_of(own_at + a * BLOCK, BLOCK), BLOCK), :] = d_ref[:, lanes].T
    fetch.wait()
    for a in range(half):
        o_ref[pl.ds(pl.multiple_of(got_at + a * BLOCK, BLOCK), BLOCK), :] = rv_ref[:, pl.ds(a * BLOCK, BLOCK)].T
    for turn in range(cycles):
        for t in range(n_blocks):
            m_ref[pl.ds(t * width, width), :] = o_ref[pl.ds(t, BLOCK, stride=n_blocks), :].T
        m_ref[...] = _apply(m_ref[...], _weights(g_ref[gate_base + 2 * turn]))
        for t in range(n_blocks):
            o_ref[pl.ds(t, BLOCK, stride=n_blocks), :] = m_ref[pl.ds(t * width, width), :].T
        tt_ref[...] = c_ref[cpl_base + turn].T
        table = tt_ref[pl.ds(col_start, width), :]
        for a in range(n_blocks):
            m_ref[pl.ds(a * width, width), :] = o_ref[pl.ds(a * BLOCK, BLOCK), :].T * table
        m_ref[...] = _apply(m_ref[...], _weights(g_ref[gate_base + 2 * turn + 1]))
        for a in range(n_blocks):
            if turn == cycles - 1:
                out_ref[:, pl.ds(a * BLOCK, BLOCK)] = m_ref[pl.ds(a * width, width), :]
            else:
                o_ref[pl.ds(a * BLOCK, BLOCK), :] = m_ref[pl.ds(a * width, width), :].T


def final_layers(parity, cut, cols, recv, gate_stack, coupling, gate_base, cpl_base, cycles):
    width, rows = cols.shape
    kernel = functools.partial(_final_kernel, gate_base=gate_base, cpl_base=cpl_base, cycles=cycles)
    out = pl.pallas_call(
        kernel,
        out_shape=jax.ShapeDtypeStruct((width, rows), cols.dtype),
        in_specs=[_smem(), _smem(), _vmem(), pl.BlockSpec(memory_space=pl.ANY), _vmem(), _vmem()],
        out_specs=_vmem(),
        scratch_shapes=[
            pltpu.VMEM((rows, width), jnp.float32),
            pltpu.VMEM((BLOCK, BLOCK), jnp.float32),
            pltpu.VMEM((BLOCK, BLOCK), jnp.float32),
            pltpu.VMEM(recv.shape, jnp.float32),
            pltpu.SemaphoreType.DMA(()),
        ],
    )(parity, cut, cols, recv, gate_stack, coupling)
    return out.T


HIGHEST_PREC = lax.Precision.HIGHEST


def partner(value, axis, distance):
    mask = 2**distance
    pairs = [(source, source ^ mask) for source in range(lax.axis_size(axis))]
    return lax.ppermute(value, axis, pairs)


def effective(weight_mat):
    order_size = weight_mat.shape[0]
    return 0.9 * jnp.eye(order_size, dtype=weight_mat.dtype) + 0.45 * weight_mat


def apply_lane(tensor, weight_mat):
    return jnp.dot(tensor, effective(weight_mat), precision=HIGHEST_PREC)


def apply_mid(tensor, weight_mat):
    order_size = weight_mat.shape[0]
    shaped = tensor.reshape(-1, order_size, tensor.shape[1])
    mixed = jnp.einsum("aic,ij->ajc", shaped, effective(weight_mat), precision=HIGHEST_PREC)
    return mixed.reshape(tensor.shape)


def apply_top(tensor, weight_mat):
    order_size = weight_mat.shape[0]
    shaped = tensor.reshape(order_size, -1)
    mixed = jnp.dot(effective(weight_mat).T, shaped, precision=HIGHEST_PREC)
    return mixed.reshape(tensor.shape)


def apply_couple(tensor, table):
    shaped = tensor.reshape(-1, table.shape[0], tensor.shape[1])
    return (shaped * table[None]).reshape(tensor.shape)


def layer_group(tensor, gate_stack, coupling, gate_base, cpl_base, cycles):
    for turn_index in range(cycles):
        first = gate_base + 3 * turn_index
        tensor = apply_top(tensor, gate_stack[first])
        tensor = apply_lane(tensor, gate_stack[first + 1])
        tensor = apply_couple(tensor, coupling[cpl_base + turn_index])
        tensor = apply_mid(tensor, gate_stack[first + 2])
    return tensor


def final_group_cols(cols, gate_stack, coupling, col_start):
    order_size = gate_stack.shape[1]
    width = cols.shape[0]
    gate_base = 3 * CYC_A + 3 * CYC_B
    cpl_base = CYC_A + CYC_B
    for turn_index in range(CYC_C):
        top_mat = effective(gate_stack[gate_base + 2 * turn_index])
        shaped = cols.reshape(width, order_size, -1)
        cols = jnp.einsum("cit,ij->cjt", shaped, top_mat, precision=HIGHEST_PREC).reshape(cols.shape)
        table = lax.dynamic_slice_in_dim(coupling[cpl_base + turn_index], col_start, width, axis=1)
        shaped = cols.reshape(width, -1, order_size)
        cols = (shaped * table.T[:, None, :]).reshape(cols.shape)
        mid_mat = effective(gate_stack[gate_base + 2 * turn_index + 1])
        cols = jnp.dot(cols.reshape(-1, order_size), mid_mat, precision=HIGHEST_PREC).reshape(cols.shape)
    return cols


def swap_bit(tensor, bit_pos):
    half_rows = tensor.shape[0] // 2
    lower = tensor[:half_rows]
    upper = tensor[half_rows:]
    parity = lax.axis_index(BITS) >> bit_pos & 1
    outgoing = jnp.where(parity == 0, upper, lower)
    incoming = partner(outgoing, BITS, bit_pos)
    return jnp.where(
        parity == 0, jnp.concatenate([lower, incoming], 0), jnp.concatenate([incoming, upper], 0)
    )


def reduce_columns(cols):
    for axis in ("x", "yl"):
        n = lax.axis_size(axis)
        blocks = cols.reshape(n, cols.shape[0] // n, cols.shape[1])
        cols = lax.all_to_all(blocks, axis, 0, 0, tiled=False).sum(0)
    return cols


def swap_lanes(cols, bit_pos):
    half = cols.shape[1] // 2
    lower = cols[:, :half]
    upper = cols[:, half:]
    parity = lax.axis_index(BITS) >> bit_pos & 1
    outgoing = jnp.where(parity == 0, upper, lower)
    incoming = partner(outgoing, BITS, bit_pos)
    return jnp.where(
        parity == 0, jnp.concatenate([lower, incoming], 1), jnp.concatenate([incoming, upper], 1)
    )


def on_device(boundary, gate_stack, coupling):
    top_bit = lax.axis_size(BITS).bit_length() - 2
    parity = (lax.axis_index(BITS) >> top_bit & 1).astype(jnp.int32).reshape(1)
    keep, send = group_a(parity, boundary[0], gate_stack, coupling, CYC_A)
    recv = partner(send, BITS, top_bit)
    cols = reduce_columns(group_b(parity, keep, recv, gate_stack, coupling, CYC_B))
    half = cols.shape[1] // 2
    low = (lax.axis_index(BITS) & 1).astype(jnp.int32).reshape(1)
    outgoing = jnp.where(low[0] == 0, cols[:, half:], cols[:, :half])
    incoming = partner(outgoing, BITS, 0)
    gate_base, cpl_base = 3 * CYC_A + 3 * CYC_B, CYC_A + CYC_B
    cut = lax.axis_index(CUTS).astype(jnp.int32).reshape(1)
    return final_layers(low, cut, cols, incoming, gate_stack, coupling, gate_base, cpl_base, CYC_C)


def solution(mesh):
    n_bits, n_cuts = mesh.shape["bits"], mesh.shape["cuts"]
    fine = Mesh(mesh.devices.reshape(2, n_bits // 4, 2, n_cuts // 4, 4), BITS + CUTS)
    in_specs = (P(CUTS, BITS, None), P(), P())
    out_specs = P(BITS, CUTS)
    return jax.shard_map(
        on_device, mesh=fine, in_specs=in_specs, out_specs=out_specs, check_vma=False
    )
```

```python
import functools

import jax
import jax.numpy as jnp
from jax import lax
from jax.experimental import pallas as pl
from jax.experimental.pallas import tpu as pltpu
from jax.sharding import Mesh, PartitionSpec as P

CYC_A = 4
CYC_B = 4
CYC_C = 5
BITS = ("yh", "z", "core")
CUTS = ("x", "yl")

BLOCK = 128


def _split(a):
    hi = a.astype(jnp.bfloat16)
    lo = (a - hi.astype(jnp.float32)).astype(jnp.bfloat16)
    return hi, lo


def _weights(g):
    hi, lo = _split(0.45 * g)
    return jnp.concatenate([hi, hi, lo], axis=0)


def _apply(x, w):
    hi, lo = _split(x)
    lhs = jnp.concatenate([hi, lo, hi], axis=1)
    return 0.9 * x + jnp.dot(lhs, w, preferred_element_type=jnp.float32)


def _weights_left(g):
    hi, lo = _split((0.45 * g).T)
    return jnp.concatenate([hi, lo, hi], axis=1)


def _apply_left(w, x):
    hi, lo = _split(x)
    rhs = jnp.concatenate([hi, hi, lo], axis=0)
    return 0.9 * x + jnp.dot(w, rhs, preferred_element_type=jnp.float32)


def _layer_turns(o_ref, t_ref, g_ref, c_ref, cycles, last_to=None):
    rows = o_ref.shape[0]
    n_blocks = rows // BLOCK
    for turn in range(cycles):
        first = 3 * turn
        table = c_ref[turn]
        xs = jnp.concatenate([o_ref[pl.ds(t, BLOCK, stride=n_blocks), :] for t in range(n_blocks)], axis=1)
        ys = _apply_left(_weights_left(g_ref[first]), xs)
        for t in range(n_blocks):
            o_ref[pl.ds(t, BLOCK, stride=n_blocks), :] = ys[:, t * BLOCK:(t + 1) * BLOCK]
        y = _apply(o_ref[...], _weights(g_ref[first + 1]))
        y = (y.reshape(n_blocks, BLOCK, -1) * table[None]).reshape(y.shape)
        if last_to is not None and turn == cycles - 1:
            for a in range(n_blocks):
                t_ref[pl.ds(a * BLOCK, BLOCK), :] = y[a * BLOCK:(a + 1) * BLOCK].T
            t_ref[...] = _apply(t_ref[...], _weights(g_ref[first + 2]))
            for a in range(n_blocks):
                last_to[:, pl.ds(a * BLOCK, BLOCK)] = t_ref[pl.ds(a * BLOCK, BLOCK), :]
        else:
            xs = jnp.concatenate([y[a * BLOCK:(a + 1) * BLOCK] for a in range(n_blocks)], axis=1)
            ys = _apply_left(_weights_left(g_ref[first + 2]), xs)
            for a in range(n_blocks):
                o_ref[pl.ds(a * BLOCK, BLOCK), :] = ys[:, a * BLOCK:(a + 1) * BLOCK]


def _group_a_kernel(p_ref, x_ref, g_ref, c_ref, keep_ref, send_ref, o_ref, *, cycles):
    half = keep_ref.shape[0]
    o_ref[...] = x_ref[...]
    _layer_turns(o_ref, None, g_ref, c_ref, cycles)
    p = p_ref[0]
    keep_ref[...] = o_ref[pl.ds(pl.multiple_of(p * half, half), half), :]
    send_ref[...] = o_ref[pl.ds(pl.multiple_of((1 - p) * half, half), half), :]


def _group_b_kernel(p_ref, keep_ref, recv_ref, g_ref, c_ref, out_ref, o_ref, t_ref, *, cycles):
    half = keep_ref.shape[0]
    p = p_ref[0]
    o_ref[pl.ds(pl.multiple_of(p * half, half), half), :] = keep_ref[...]
    o_ref[pl.ds(pl.multiple_of((1 - p) * half, half), half), :] = recv_ref[...]
    _layer_turns(o_ref, t_ref, g_ref, c_ref, cycles, last_to=out_ref)


def _smem():
    return pl.BlockSpec(memory_space=pltpu.SMEM)


def _vmem():
    return pl.BlockSpec(memory_space=pltpu.VMEM)


def _stack_block(count, index):
    return pl.BlockSpec((count, BLOCK, BLOCK), lambda step: (index, 0, 0), memory_space=pltpu.VMEM)


def group_a(parity, x, gate_stack, coupling, cycles):
    half = jax.ShapeDtypeStruct((x.shape[0] // 2, x.shape[1]), x.dtype)
    return pl.pallas_call(
        functools.partial(_group_a_kernel, cycles=cycles),
        out_shape=(half, half),
        grid=(1,),
        in_specs=[_smem(), _vmem(), _stack_block(3 * cycles, 0), _stack_block(cycles, 0)],
        out_specs=(_vmem(), _vmem()),
        scratch_shapes=[pltpu.VMEM(x.shape, jnp.float32)],
    )(parity, x, gate_stack, coupling)


def group_b(parity, keep, recv, gate_stack, coupling, cycles):
    rows, cols = keep.shape[0] * 2, keep.shape[1]
    return pl.pallas_call(
        functools.partial(_group_b_kernel, cycles=cycles),
        out_shape=jax.ShapeDtypeStruct((cols, rows), keep.dtype),
        grid=(1,),
        in_specs=[_smem(), _vmem(), _vmem(), _stack_block(3 * cycles, 1), _stack_block(cycles, 1)],
        out_specs=_vmem(),
        scratch_shapes=[pltpu.VMEM((rows, cols), jnp.float32), pltpu.VMEM((rows, cols), jnp.float32)],
    )(parity, keep, recv, gate_stack, coupling)


def _final_kernel(p_ref, cut_ref, d_ref, recv_hbm, g_ref, c_ref, out_ref, o_ref, m_ref, tt_ref, rv_ref, sem, *,
                  gate_base, cpl_base, cycles):
    width = d_ref.shape[0]
    n_blocks = d_ref.shape[1] // BLOCK
    half = n_blocks // 2
    half_rows = half * BLOCK
    p = p_ref[0]
    col_start = pl.multiple_of(cut_ref[0] * width, width)
    fetch = pltpu.make_async_copy(recv_hbm, rv_ref, sem)
    fetch.start()
    own_at = pl.multiple_of(p * half_rows, half_rows)
    got_at = pl.multiple_of((1 - p) * half_rows, half_rows)
    for a in range(half):
        lanes = pl.ds(pl.multiple_of(own_at + a * BLOCK, BLOCK), BLOCK)
        o_ref[pl.ds(pl.multiple_of(own_at + a * BLOCK, BLOCK), BLOCK), :] = d_ref[:, lanes].T
    fetch.wait()
    for a in range(half):
        o_ref[pl.ds(pl.multiple_of(got_at + a * BLOCK, BLOCK), BLOCK), :] = rv_ref[:, pl.ds(a * BLOCK, BLOCK)].T
    for turn in range(cycles):
        for t in range(n_blocks):
            m_ref[pl.ds(t * width, width), :] = o_ref[pl.ds(t, BLOCK, stride=n_blocks), :].T
        m_ref[...] = _apply(m_ref[...], _weights(g_ref[gate_base + 2 * turn]))
        for t in range(n_blocks):
            o_ref[pl.ds(t, BLOCK, stride=n_blocks), :] = m_ref[pl.ds(t * width, width), :].T
        tt_ref[...] = c_ref[cpl_base + turn].T
        table = tt_ref[pl.ds(col_start, width), :]
        for a in range(n_blocks):
            m_ref[pl.ds(a * width, width), :] = o_ref[pl.ds(a * BLOCK, BLOCK), :].T * table
        m_ref[...] = _apply(m_ref[...], _weights(g_ref[gate_base + 2 * turn + 1]))
        for a in range(n_blocks):
            if turn == cycles - 1:
                out_ref[:, pl.ds(a * BLOCK, BLOCK)] = m_ref[pl.ds(a * width, width), :]
            else:
                o_ref[pl.ds(a * BLOCK, BLOCK), :] = m_ref[pl.ds(a * width, width), :].T


def final_layers(parity, cut, cols, recv, gate_stack, coupling, gate_base, cpl_base, cycles):
    width, rows = cols.shape
    kernel = functools.partial(_final_kernel, gate_base=gate_base, cpl_base=cpl_base, cycles=cycles)
    out = pl.pallas_call(
        kernel,
        out_shape=jax.ShapeDtypeStruct((width, rows), cols.dtype),
        in_specs=[_smem(), _smem(), _vmem(), pl.BlockSpec(memory_space=pl.ANY), _vmem(), _vmem()],
        out_specs=_vmem(),
        scratch_shapes=[
            pltpu.VMEM((rows, width), jnp.float32),
            pltpu.VMEM((BLOCK, BLOCK), jnp.float32),
            pltpu.VMEM((BLOCK, BLOCK), jnp.float32),
            pltpu.VMEM(recv.shape, jnp.float32),
            pltpu.SemaphoreType.DMA(()),
        ],
    )(parity, cut, cols, recv, gate_stack, coupling)
    return out.T


HIGHEST_PREC = lax.Precision.HIGHEST


def partner(value, axis, distance):
    mask = 2**distance
    pairs = [(source, source ^ mask) for source in range(lax.axis_size(axis))]
    return lax.ppermute(value, axis, pairs)


def effective(weight_mat):
    order_size = weight_mat.shape[0]
    return 0.9 * jnp.eye(order_size, dtype=weight_mat.dtype) + 0.45 * weight_mat


def apply_lane(tensor, weight_mat):
    return jnp.dot(tensor, effective(weight_mat), precision=HIGHEST_PREC)


def apply_mid(tensor, weight_mat):
    order_size = weight_mat.shape[0]
    shaped = tensor.reshape(-1, order_size, tensor.shape[1])
    mixed = jnp.einsum("aic,ij->ajc", shaped, effective(weight_mat), precision=HIGHEST_PREC)
    return mixed.reshape(tensor.shape)


def apply_top(tensor, weight_mat):
    order_size = weight_mat.shape[0]
    shaped = tensor.reshape(order_size, -1)
    mixed = jnp.dot(effective(weight_mat).T, shaped, precision=HIGHEST_PREC)
    return mixed.reshape(tensor.shape)


def apply_couple(tensor, table):
    shaped = tensor.reshape(-1, table.shape[0], tensor.shape[1])
    return (shaped * table[None]).reshape(tensor.shape)


def layer_group(tensor, gate_stack, coupling, gate_base, cpl_base, cycles):
    for turn_index in range(cycles):
        first = gate_base + 3 * turn_index
        tensor = apply_top(tensor, gate_stack[first])
        tensor = apply_lane(tensor, gate_stack[first + 1])
        tensor = apply_couple(tensor, coupling[cpl_base + turn_index])
        tensor = apply_mid(tensor, gate_stack[first + 2])
    return tensor


def final_group_cols(cols, gate_stack, coupling, col_start):
    order_size = gate_stack.shape[1]
    width = cols.shape[0]
    gate_base = 3 * CYC_A + 3 * CYC_B
    cpl_base = CYC_A + CYC_B
    for turn_index in range(CYC_C):
        top_mat = effective(gate_stack[gate_base + 2 * turn_index])
        shaped = cols.reshape(width, order_size, -1)
        cols = jnp.einsum("cit,ij->cjt", shaped, top_mat, precision=HIGHEST_PREC).reshape(cols.shape)
        table = lax.dynamic_slice_in_dim(coupling[cpl_base + turn_index], col_start, width, axis=1)
        shaped = cols.reshape(width, -1, order_size)
        cols = (shaped * table.T[:, None, :]).reshape(cols.shape)
        mid_mat = effective(gate_stack[gate_base + 2 * turn_index + 1])
        cols = jnp.dot(cols.reshape(-1, order_size), mid_mat, precision=HIGHEST_PREC).reshape(cols.shape)
    return cols


def swap_bit(tensor, bit_pos):
    half_rows = tensor.shape[0] // 2
    lower = tensor[:half_rows]
    upper = tensor[half_rows:]
    parity = lax.axis_index(BITS) >> bit_pos & 1
    outgoing = jnp.where(parity == 0, upper, lower)
    incoming = partner(outgoing, BITS, bit_pos)
    return jnp.where(
        parity == 0, jnp.concatenate([lower, incoming], 0), jnp.concatenate([incoming, upper], 0)
    )


def reduce_columns(cols):
    for axis in ("x", "yl"):
        n = lax.axis_size(axis)
        blocks = cols.reshape(n, cols.shape[0] // n, cols.shape[1])
        cols = lax.all_to_all(blocks, axis, 0, 0, tiled=False).sum(0)
    return cols


def swap_lanes(cols, bit_pos):
    half = cols.shape[1] // 2
    lower = cols[:, :half]
    upper = cols[:, half:]
    parity = lax.axis_index(BITS) >> bit_pos & 1
    outgoing = jnp.where(parity == 0, upper, lower)
    incoming = partner(outgoing, BITS, bit_pos)
    return jnp.where(
        parity == 0, jnp.concatenate([lower, incoming], 1), jnp.concatenate([incoming, upper], 1)
    )


def on_device(boundary, gate_stack, coupling):
    top_bit = lax.axis_size(BITS).bit_length() - 2
    parity = (lax.axis_index(BITS) >> top_bit & 1).astype(jnp.int32).reshape(1)
    keep, send = group_a(parity, boundary[0], gate_stack, coupling, CYC_A)
    recv = partner(send, BITS, top_bit)
    cols = reduce_columns(group_b(parity, keep, recv, gate_stack, coupling, CYC_B))
    half = cols.shape[1] // 2
    low = (lax.axis_index(BITS) & 1).astype(jnp.int32).reshape(1)
    outgoing = jnp.where(low[0] == 0, cols[:, half:], cols[:, :half])
    incoming = partner(outgoing, BITS, 0)
    gate_base, cpl_base = 3 * CYC_A + 3 * CYC_B, CYC_A + CYC_B
    cut = lax.axis_index(CUTS).astype(jnp.int32).reshape(1)
    return final_layers(low, cut, cols, incoming, gate_stack, coupling, gate_base, cpl_base, CYC_C)


def solution(mesh):
    n_bits, n_cuts = mesh.shape["bits"], mesh.shape["cuts"]
    fine = Mesh(mesh.devices.reshape(2, n_bits // 4, 2, n_cuts // 4, 4), BITS + CUTS)
    in_specs = (P(CUTS, BITS, None), P(), P())
    out_specs = P(BITS, CUTS)
    return jax.shard_map(
        on_device, mesh=fine, in_specs=in_specs, out_specs=out_specs, check_vma=False
    )
```

```python
import functools

import jax
import jax.numpy as jnp
from jax import lax
from jax.experimental import pallas as pl
from jax.experimental.pallas import tpu as pltpu
from jax.sharding import Mesh, PartitionSpec as P

CYC_A = 4
CYC_B = 4
CYC_C = 5
BITS = ("yh", "z", "core")
CUTS = ("x", "yl")

BLOCK = 128


def _split(a):
    hi = a.astype(jnp.bfloat16)
    lo = (a - hi.astype(jnp.float32)).astype(jnp.bfloat16)
    return hi, lo


def _weights(g):
    hi, lo = _split(0.45 * g)
    return jnp.concatenate([hi, hi, lo], axis=0)


def _apply(x, w):
    hi, lo = _split(x)
    lhs = jnp.concatenate([hi, lo, hi], axis=1)
    return 0.9 * x + jnp.dot(lhs, w, preferred_element_type=jnp.float32)


def _weights_left(g):
    hi, lo = _split((0.45 * g).T)
    return jnp.concatenate([hi, lo, hi], axis=1)


def _apply_left(w, x):
    hi, lo = _split(x)
    rhs = jnp.concatenate([hi, hi, lo], axis=0)
    return 0.9 * x + jnp.dot(w, rhs, preferred_element_type=jnp.float32)


def _layer_turns(o_ref, t_ref, g_ref, c_ref, cycles, last_to=None):
    rows = o_ref.shape[0]
    n_blocks = rows // BLOCK
    for turn in range(cycles):
        first = 3 * turn
        table = c_ref[turn]
        xs = jnp.concatenate([o_ref[pl.ds(t, BLOCK, stride=n_blocks), :] for t in range(n_blocks)], axis=1)
        ys = _apply_left(_weights_left(g_ref[first]), xs)
        for t in range(n_blocks):
            o_ref[pl.ds(t, BLOCK, stride=n_blocks), :] = ys[:, t * BLOCK:(t + 1) * BLOCK]
        y = _apply(o_ref[...], _weights(g_ref[first + 1]))
        o_ref[...] = (y.reshape(n_blocks, BLOCK, -1) * table[None]).reshape(y.shape)
        if last_to is not None and turn == cycles - 1:
            for a in range(n_blocks):
                t_ref[pl.ds(a * BLOCK, BLOCK), :] = o_ref[pl.ds(a * BLOCK, BLOCK), :].T
            t_ref[...] = _apply(t_ref[...], _weights(g_ref[first + 2]))
            for a in range(n_blocks):
                last_to[:, pl.ds(a * BLOCK, BLOCK)] = t_ref[pl.ds(a * BLOCK, BLOCK), :]
        else:
            xs = jnp.concatenate([o_ref[pl.ds(a * BLOCK, BLOCK), :] for a in range(n_blocks)], axis=1)
            ys = _apply_left(_weights_left(g_ref[first + 2]), xs)
            for a in range(n_blocks):
                o_ref[pl.ds(a * BLOCK, BLOCK), :] = ys[:, a * BLOCK:(a + 1) * BLOCK]


def _group_a_kernel(p_ref, x_ref, g_ref, c_ref, keep_ref, send_ref, o_ref, *, cycles):
    half = keep_ref.shape[0]
    o_ref[...] = x_ref[...]
    _layer_turns(o_ref, None, g_ref, c_ref, cycles)
    p = p_ref[0]
    keep_ref[...] = o_ref[pl.ds(pl.multiple_of(p * half, half), half), :]
    send_ref[...] = o_ref[pl.ds(pl.multiple_of((1 - p) * half, half), half), :]


def _group_b_kernel(p_ref, keep_ref, recv_hbm, g_ref, c_ref, out_ref, o_ref, t_ref, sem, *, cycles):
    half = keep_ref.shape[0]
    p = p_ref[0]
    fetch = pltpu.make_async_copy(recv_hbm, o_ref.at[pl.ds(pl.multiple_of((1 - p) * half, half), half), :], sem)
    fetch.start()
    o_ref[pl.ds(pl.multiple_of(p * half, half), half), :] = keep_ref[...]
    fetch.wait()
    _layer_turns(o_ref, t_ref, g_ref, c_ref, cycles, last_to=out_ref)


def _smem():
    return pl.BlockSpec(memory_space=pltpu.SMEM)


def _vmem():
    return pl.BlockSpec(memory_space=pltpu.VMEM)


def _stack_block(count, index):
    return pl.BlockSpec((count, BLOCK, BLOCK), lambda step: (index, 0, 0), memory_space=pltpu.VMEM)


def group_a(parity, x, gate_stack, coupling, cycles):
    half = jax.ShapeDtypeStruct((x.shape[0] // 2, x.shape[1]), x.dtype)
    return pl.pallas_call(
        functools.partial(_group_a_kernel, cycles=cycles),
        out_shape=(half, half),
        grid=(1,),
        in_specs=[_smem(), _vmem(), _stack_block(3 * cycles, 0), _stack_block(cycles, 0)],
        out_specs=(_vmem(), _vmem()),
        scratch_shapes=[pltpu.VMEM(x.shape, jnp.float32)],
    )(parity, x, gate_stack, coupling)


def group_b(parity, keep, recv, gate_stack, coupling, cycles):
    rows, cols = keep.shape[0] * 2, keep.shape[1]
    return pl.pallas_call(
        functools.partial(_group_b_kernel, cycles=cycles),
        out_shape=jax.ShapeDtypeStruct((cols, rows), keep.dtype),
        grid=(1,),
        in_specs=[_smem(), _vmem(), pl.BlockSpec(memory_space=pltpu.HBM), _stack_block(3 * cycles, 1),
                  _stack_block(cycles, 1)],
        out_specs=_vmem(),
        scratch_shapes=[
            pltpu.VMEM((rows, cols), jnp.float32),
            pltpu.VMEM((rows, cols), jnp.float32),
            pltpu.SemaphoreType.DMA(()),
        ],
    )(parity, keep, recv, gate_stack, coupling)


def _final_kernel(d_ref, g_ref, tab_ref, out_ref, o_ref, m_ref, *, gate_base, cycles):
    width = d_ref.shape[0]
    n_blocks = d_ref.shape[1] // BLOCK
    for a in range(n_blocks):
        o_ref[pl.ds(a * BLOCK, BLOCK), :] = d_ref[:, pl.ds(a * BLOCK, BLOCK)].T
    for turn in range(cycles):
        for t in range(n_blocks):
            m_ref[pl.ds(t * width, width), :] = o_ref[pl.ds(t, BLOCK, stride=n_blocks), :].T
        m_ref[...] = _apply(m_ref[...], _weights(g_ref[gate_base + 2 * turn]))
        for t in range(n_blocks):
            o_ref[pl.ds(t, BLOCK, stride=n_blocks), :] = m_ref[pl.ds(t * width, width), :].T
        table = tab_ref[turn]
        for a in range(n_blocks):
            m_ref[pl.ds(a * width, width), :] = o_ref[pl.ds(a * BLOCK, BLOCK), :].T * table
        m_ref[...] = _apply(m_ref[...], _weights(g_ref[gate_base + 2 * turn + 1]))
        for a in range(n_blocks):
            if turn == cycles - 1:
                out_ref[:, pl.ds(a * BLOCK, BLOCK)] = m_ref[pl.ds(a * width, width), :]
            else:
                o_ref[pl.ds(a * BLOCK, BLOCK), :] = m_ref[pl.ds(a * width, width), :].T


def final_layers(d, gate_stack, tables, gate_base, cycles):
    width, rows = d.shape
    kernel = functools.partial(_final_kernel, gate_base=gate_base, cycles=cycles)
    out = pl.pallas_call(
        kernel,
        out_shape=jax.ShapeDtypeStruct((width, rows), d.dtype),
        scratch_shapes=[pltpu.VMEM((rows, width), jnp.float32), pltpu.VMEM((BLOCK, BLOCK), jnp.float32)],
    )(d, gate_stack, tables)
    return out.T


HIGHEST_PREC = lax.Precision.HIGHEST


def partner(value, axis, distance):
    mask = 2**distance
    pairs = [(source, source ^ mask) for source in range(lax.axis_size(axis))]
    return lax.ppermute(value, axis, pairs)


def effective(weight_mat):
    order_size = weight_mat.shape[0]
    return 0.9 * jnp.eye(order_size, dtype=weight_mat.dtype) + 0.45 * weight_mat


def apply_lane(tensor, weight_mat):
    return jnp.dot(tensor, effective(weight_mat), precision=HIGHEST_PREC)


def apply_mid(tensor, weight_mat):
    order_size = weight_mat.shape[0]
    shaped = tensor.reshape(-1, order_size, tensor.shape[1])
    mixed = jnp.einsum("aic,ij->ajc", shaped, effective(weight_mat), precision=HIGHEST_PREC)
    return mixed.reshape(tensor.shape)


def apply_top(tensor, weight_mat):
    order_size = weight_mat.shape[0]
    shaped = tensor.reshape(order_size, -1)
    mixed = jnp.dot(effective(weight_mat).T, shaped, precision=HIGHEST_PREC)
    return mixed.reshape(tensor.shape)


def apply_couple(tensor, table):
    shaped = tensor.reshape(-1, table.shape[0], tensor.shape[1])
    return (shaped * table[None]).reshape(tensor.shape)


def layer_group(tensor, gate_stack, coupling, gate_base, cpl_base, cycles):
    for turn_index in range(cycles):
        first = gate_base + 3 * turn_index
        tensor = apply_top(tensor, gate_stack[first])
        tensor = apply_lane(tensor, gate_stack[first + 1])
        tensor = apply_couple(tensor, coupling[cpl_base + turn_index])
        tensor = apply_mid(tensor, gate_stack[first + 2])
    return tensor


def final_group_cols(cols, gate_stack, coupling, col_start):
    order_size = gate_stack.shape[1]
    width = cols.shape[0]
    gate_base = 3 * CYC_A + 3 * CYC_B
    cpl_base = CYC_A + CYC_B
    for turn_index in range(CYC_C):
        top_mat = effective(gate_stack[gate_base + 2 * turn_index])
        shaped = cols.reshape(width, order_size, -1)
        cols = jnp.einsum("cit,ij->cjt", shaped, top_mat, precision=HIGHEST_PREC).reshape(cols.shape)
        table = lax.dynamic_slice_in_dim(coupling[cpl_base + turn_index], col_start, width, axis=1)
        shaped = cols.reshape(width, -1, order_size)
        cols = (shaped * table.T[:, None, :]).reshape(cols.shape)
        mid_mat = effective(gate_stack[gate_base + 2 * turn_index + 1])
        cols = jnp.dot(cols.reshape(-1, order_size), mid_mat, precision=HIGHEST_PREC).reshape(cols.shape)
    return cols


def swap_bit(tensor, bit_pos):
    half_rows = tensor.shape[0] // 2
    lower = tensor[:half_rows]
    upper = tensor[half_rows:]
    parity = lax.axis_index(BITS) >> bit_pos & 1
    outgoing = jnp.where(parity == 0, upper, lower)
    incoming = partner(outgoing, BITS, bit_pos)
    return jnp.where(
        parity == 0, jnp.concatenate([lower, incoming], 0), jnp.concatenate([incoming, upper], 0)
    )


def reduce_columns(cols):
    for axis in ("x", "yl"):
        n = lax.axis_size(axis)
        blocks = cols.reshape(n, cols.shape[0] // n, cols.shape[1])
        cols = lax.all_to_all(blocks, axis, 0, 0, tiled=False).sum(0)
    return cols


def swap_lanes(cols, bit_pos):
    half = cols.shape[1] // 2
    lower = cols[:, :half]
    upper = cols[:, half:]
    parity = lax.axis_index(BITS) >> bit_pos & 1
    outgoing = jnp.where(parity == 0, upper, lower)
    incoming = partner(outgoing, BITS, bit_pos)
    return jnp.where(
        parity == 0, jnp.concatenate([lower, incoming], 1), jnp.concatenate([incoming, upper], 1)
    )


def on_device(boundary, gate_stack, coupling):
    top_bit = lax.axis_size(BITS).bit_length() - 2
    parity = (lax.axis_index(BITS) >> top_bit & 1).astype(jnp.int32).reshape(1)
    keep, send = group_a(parity, boundary[0], gate_stack, coupling, CYC_A)
    recv = partner(send, BITS, top_bit)
    cols = group_b(parity, keep, recv, gate_stack, coupling, CYC_B)
    cols = swap_lanes(reduce_columns(cols), 0)
    width = cols.shape[0]
    col_start = lax.axis_index(CUTS) * width
    cpl_base = CYC_A + CYC_B
    tables = lax.dynamic_slice_in_dim(coupling[cpl_base:cpl_base + CYC_C], col_start, width, axis=2)
    return final_layers(cols, gate_stack, jnp.swapaxes(tables, 1, 2), 3 * CYC_A + 3 * CYC_B, CYC_C)


def solution(mesh):
    n_bits, n_cuts = mesh.shape["bits"], mesh.shape["cuts"]
    fine = Mesh(mesh.devices.reshape(2, n_bits // 4, 2, n_cuts // 4, 4), BITS + CUTS)
    in_specs = (P(CUTS, BITS, None), P(), P())
    out_specs = P(BITS, CUTS)
    return jax.shard_map(
        on_device, mesh=fine, in_specs=in_specs, out_specs=out_specs, check_vma=False
    )
```

```python
import functools

import jax
import jax.numpy as jnp
from jax import lax
from jax.experimental import pallas as pl
from jax.experimental.pallas import tpu as pltpu
from jax.sharding import Mesh, PartitionSpec as P

CYC_A = 4
CYC_B = 4
CYC_C = 5
BITS = ("yh", "z", "core")
CUTS = ("x", "yl")

BLOCK = 128


def _split(a):
    hi = a.astype(jnp.bfloat16)
    lo = (a - hi.astype(jnp.float32)).astype(jnp.bfloat16)
    return hi, lo


def _weights(g):
    hi, lo = _split(0.45 * g)
    return jnp.concatenate([hi, hi, lo], axis=0)


def _apply(x, w):
    hi, lo = _split(x)
    lhs = jnp.concatenate([hi, lo, hi], axis=1)
    return 0.9 * x + jnp.dot(lhs, w, preferred_element_type=jnp.float32)


def _weights_left(g):
    hi, lo = _split((0.45 * g).T)
    return jnp.concatenate([hi, lo, hi], axis=1)


def _apply_left(w, x):
    hi, lo = _split(x)
    rhs = jnp.concatenate([hi, hi, lo], axis=0)
    return 0.9 * x + jnp.dot(w, rhs, preferred_element_type=jnp.float32)


def _layer_turns(o_ref, t_ref, g_ref, c_ref, cycles, last_to=None):
    rows = o_ref.shape[0]
    n_blocks = rows // BLOCK
    for turn in range(cycles):
        first = 3 * turn
        table = c_ref[turn]
        xs = jnp.concatenate([o_ref[pl.ds(t, BLOCK, stride=n_blocks), :] for t in range(n_blocks)], axis=1)
        ys = _apply_left(_weights_left(g_ref[first]), xs)
        for t in range(n_blocks):
            o_ref[pl.ds(t, BLOCK, stride=n_blocks), :] = ys[:, t * BLOCK:(t + 1) * BLOCK]
        y = _apply(o_ref[...], _weights(g_ref[first + 1]))
        o_ref[...] = (y.reshape(n_blocks, BLOCK, -1) * table[None]).reshape(y.shape)
        if last_to is not None and turn == cycles - 1:
            for a in range(n_blocks):
                t_ref[pl.ds(a * BLOCK, BLOCK), :] = o_ref[pl.ds(a * BLOCK, BLOCK), :].T
            t_ref[...] = _apply(t_ref[...], _weights(g_ref[first + 2]))
            for a in range(n_blocks):
                last_to[:, pl.ds(a * BLOCK, BLOCK)] = t_ref[pl.ds(a * BLOCK, BLOCK), :]
        else:
            xs = jnp.concatenate([o_ref[pl.ds(a * BLOCK, BLOCK), :] for a in range(n_blocks)], axis=1)
            ys = _apply_left(_weights_left(g_ref[first + 2]), xs)
            for a in range(n_blocks):
                o_ref[pl.ds(a * BLOCK, BLOCK), :] = ys[:, a * BLOCK:(a + 1) * BLOCK]


def _group_a_kernel(p_ref, x_ref, g_ref, c_ref, keep_ref, send_ref, o_ref, *, cycles):
    half = keep_ref.shape[0]
    o_ref[...] = x_ref[...]
    _layer_turns(o_ref, None, g_ref, c_ref, cycles)
    p = p_ref[0]
    keep_ref[...] = o_ref[pl.ds(pl.multiple_of(p * half, half), half), :]
    send_ref[...] = o_ref[pl.ds(pl.multiple_of((1 - p) * half, half), half), :]


def _group_b_kernel(p_ref, keep_ref, recv_ref, g_ref, c_ref, out_ref, o_ref, t_ref, *, cycles):
    half = keep_ref.shape[0]
    p = p_ref[0]
    o_ref[pl.ds(pl.multiple_of(p * half, half), half), :] = keep_ref[...]
    o_ref[pl.ds(pl.multiple_of((1 - p) * half, half), half), :] = recv_ref[...]
    _layer_turns(o_ref, t_ref, g_ref, c_ref, cycles, last_to=out_ref)


def _smem():
    return pl.BlockSpec(memory_space=pltpu.SMEM)


def _vmem():
    return pl.BlockSpec(memory_space=pltpu.VMEM)


def _stack_block(count, index):
    return pl.BlockSpec((count, BLOCK, BLOCK), lambda step: (index, 0, 0), memory_space=pltpu.VMEM)


def group_a(parity, x, gate_stack, coupling, cycles):
    half = jax.ShapeDtypeStruct((x.shape[0] // 2, x.shape[1]), x.dtype)
    return pl.pallas_call(
        functools.partial(_group_a_kernel, cycles=cycles),
        out_shape=(half, half),
        grid=(1,),
        in_specs=[_smem(), _vmem(), _stack_block(3 * cycles, 0), _stack_block(cycles, 0)],
        out_specs=(_vmem(), _vmem()),
        scratch_shapes=[pltpu.VMEM(x.shape, jnp.float32)],
    )(parity, x, gate_stack, coupling)


def group_b(parity, keep, recv, gate_stack, coupling, cycles):
    rows, cols = keep.shape[0] * 2, keep.shape[1]
    return pl.pallas_call(
        functools.partial(_group_b_kernel, cycles=cycles),
        out_shape=jax.ShapeDtypeStruct((cols, rows), keep.dtype),
        grid=(1,),
        in_specs=[_smem(), _vmem(), _vmem(), _stack_block(3 * cycles, 1), _stack_block(cycles, 1)],
        out_specs=_vmem(),
        scratch_shapes=[pltpu.VMEM((rows, cols), jnp.float32), pltpu.VMEM((rows, cols), jnp.float32)],
    )(parity, keep, recv, gate_stack, coupling)


def _final_kernel(d_ref, g_ref, tab_ref, out_ref, o_ref, m_ref, *, gate_base, cycles):
    width = d_ref.shape[0]
    n_blocks = d_ref.shape[1] // BLOCK
    for a in range(n_blocks):
        o_ref[pl.ds(a * BLOCK, BLOCK), :] = d_ref[:, pl.ds(a * BLOCK, BLOCK)].T
    for turn in range(cycles):
        for t in range(n_blocks):
            m_ref[pl.ds(t * width, width), :] = o_ref[pl.ds(t, BLOCK, stride=n_blocks), :].T
        m_ref[...] = _apply(m_ref[...], _weights(g_ref[gate_base + 2 * turn]))
        for t in range(n_blocks):
            o_ref[pl.ds(t, BLOCK, stride=n_blocks), :] = m_ref[pl.ds(t * width, width), :].T
        table = tab_ref[turn]
        for a in range(n_blocks):
            m_ref[pl.ds(a * width, width), :] = o_ref[pl.ds(a * BLOCK, BLOCK), :].T * table
        m_ref[...] = _apply(m_ref[...], _weights(g_ref[gate_base + 2 * turn + 1]))
        for a in range(n_blocks):
            if turn == cycles - 1:
                out_ref[:, pl.ds(a * BLOCK, BLOCK)] = m_ref[pl.ds(a * width, width), :]
            else:
                o_ref[pl.ds(a * BLOCK, BLOCK), :] = m_ref[pl.ds(a * width, width), :].T


def final_layers(d, gate_stack, tables, gate_base, cycles):
    width, rows = d.shape
    kernel = functools.partial(_final_kernel, gate_base=gate_base, cycles=cycles)
    out = pl.pallas_call(
        kernel,
        out_shape=jax.ShapeDtypeStruct((width, rows), d.dtype),
        scratch_shapes=[pltpu.VMEM((rows, width), jnp.float32), pltpu.VMEM((BLOCK, BLOCK), jnp.float32)],
    )(d, gate_stack, tables)
    return out.T


HIGHEST_PREC = lax.Precision.HIGHEST


def partner(value, axis, distance):
    mask = 2**distance
    pairs = [(source, source ^ mask) for source in range(lax.axis_size(axis))]
    return lax.ppermute(value, axis, pairs)


def effective(weight_mat):
    order_size = weight_mat.shape[0]
    return 0.9 * jnp.eye(order_size, dtype=weight_mat.dtype) + 0.45 * weight_mat


def apply_lane(tensor, weight_mat):
    return jnp.dot(tensor, effective(weight_mat), precision=HIGHEST_PREC)


def apply_mid(tensor, weight_mat):
    order_size = weight_mat.shape[0]
    shaped = tensor.reshape(-1, order_size, tensor.shape[1])
    mixed = jnp.einsum("aic,ij->ajc", shaped, effective(weight_mat), precision=HIGHEST_PREC)
    return mixed.reshape(tensor.shape)


def apply_top(tensor, weight_mat):
    order_size = weight_mat.shape[0]
    shaped = tensor.reshape(order_size, -1)
    mixed = jnp.dot(effective(weight_mat).T, shaped, precision=HIGHEST_PREC)
    return mixed.reshape(tensor.shape)


def apply_couple(tensor, table):
    shaped = tensor.reshape(-1, table.shape[0], tensor.shape[1])
    return (shaped * table[None]).reshape(tensor.shape)


def layer_group(tensor, gate_stack, coupling, gate_base, cpl_base, cycles):
    for turn_index in range(cycles):
        first = gate_base + 3 * turn_index
        tensor = apply_top(tensor, gate_stack[first])
        tensor = apply_lane(tensor, gate_stack[first + 1])
        tensor = apply_couple(tensor, coupling[cpl_base + turn_index])
        tensor = apply_mid(tensor, gate_stack[first + 2])
    return tensor


def final_group_cols(cols, gate_stack, coupling, col_start):
    order_size = gate_stack.shape[1]
    width = cols.shape[0]
    gate_base = 3 * CYC_A + 3 * CYC_B
    cpl_base = CYC_A + CYC_B
    for turn_index in range(CYC_C):
        top_mat = effective(gate_stack[gate_base + 2 * turn_index])
        shaped = cols.reshape(width, order_size, -1)
        cols = jnp.einsum("cit,ij->cjt", shaped, top_mat, precision=HIGHEST_PREC).reshape(cols.shape)
        table = lax.dynamic_slice_in_dim(coupling[cpl_base + turn_index], col_start, width, axis=1)
        shaped = cols.reshape(width, -1, order_size)
        cols = (shaped * table.T[:, None, :]).reshape(cols.shape)
        mid_mat = effective(gate_stack[gate_base + 2 * turn_index + 1])
        cols = jnp.dot(cols.reshape(-1, order_size), mid_mat, precision=HIGHEST_PREC).reshape(cols.shape)
    return cols


def swap_bit(tensor, bit_pos):
    half_rows = tensor.shape[0] // 2
    lower = tensor[:half_rows]
    upper = tensor[half_rows:]
    parity = lax.axis_index(BITS) >> bit_pos & 1
    outgoing = jnp.where(parity == 0, upper, lower)
    incoming = partner(outgoing, BITS, bit_pos)
    return jnp.where(
        parity == 0, jnp.concatenate([lower, incoming], 0), jnp.concatenate([incoming, upper], 0)
    )


def reduce_columns(cols):
    for axis in ("x", "yl"):
        n = lax.axis_size(axis)
        blocks = cols.reshape(n, cols.shape[0] // n, cols.shape[1])
        cols = lax.all_to_all(blocks, axis, 0, 0, tiled=False).sum(0)
    return cols


def swap_lanes(cols, bit_pos):
    half = cols.shape[1] // 2
    lower = cols[:, :half]
    upper = cols[:, half:]
    parity = lax.axis_index(BITS) >> bit_pos & 1
    outgoing = jnp.where(parity == 0, upper, lower)
    incoming = partner(outgoing, BITS, bit_pos)
    return jnp.where(
        parity == 0, jnp.concatenate([lower, incoming], 1), jnp.concatenate([incoming, upper], 1)
    )


def on_device(boundary, gate_stack, coupling):
    top_bit = lax.axis_size(BITS).bit_length() - 2
    parity = (lax.axis_index(BITS) >> top_bit & 1).astype(jnp.int32).reshape(1)
    keep, send = group_a(parity, boundary[0], gate_stack, coupling, CYC_A)
    recv = partner(send, BITS, top_bit)
    width = boundary.shape[2] // lax.axis_size(CUTS)
    col_start = lax.axis_index(CUTS) * width
    cpl_base = CYC_A + CYC_B
    tables = lax.dynamic_slice_in_dim(coupling[cpl_base:cpl_base + CYC_C], col_start, width, axis=2)
    tables, recv = lax.optimization_barrier((jnp.swapaxes(tables, 1, 2), recv))
    cols = group_b(parity, keep, recv, gate_stack, coupling, CYC_B)
    cols = swap_lanes(reduce_columns(cols), 0)
    return final_layers(cols, gate_stack, tables, 3 * CYC_A + 3 * CYC_B, CYC_C)


def solution(mesh):
    n_bits, n_cuts = mesh.shape["bits"], mesh.shape["cuts"]
    fine = Mesh(mesh.devices.reshape(2, n_bits // 4, 2, n_cuts // 4, 4), BITS + CUTS)
    in_specs = (P(CUTS, BITS, None), P(), P())
    out_specs = P(BITS, CUTS)
    return jax.shard_map(
        on_device, mesh=fine, in_specs=in_specs, out_specs=out_specs, check_vma=False
    )
```
